32 devices in a mesh: region: 4 (over y, x), tile: 8 (over z, core).
Axes of the slice: x: 2, y: 2, z: 4, core: 2. Of those that a mesh axis runs over, the one named last changes fastest.
Arguments:
- estimate: float32 [32, 128, 512], P('region', 'tile'), may hold values from 0.5 to 18
- observed: float32 [32, 16, 32, 512], P('region', 'tile'), may hold values from 0.3 to 3
- tile_offset: int32 [16], P('tile'), may hold values from 0 to 96
- tile_view: int32 [16], P('tile'), may hold values from 0 to 5
- psf_taps: float32 [6, 3, 3, 15], replicated, may hold values from 0.01 to 0.1
- view_weight: float32 [6], replicated, may hold values from 0.5 to 2
Outputs:
- updated: float32 [32, 128, 512], P('region', 'tile')
The draws below stay inside these ranges and needn't reach their ends.
All inputs are finite; a program needn't handle non-finite values.
Results may differ from the reference program's by a relative error of at most 0.0003.
Values sent between devices are 32-bit elements; how exact they have to be, the bound alone decides.
No kernel may reach another device: no remote copies, remote signals or barrier semaphores. Data moves between devices by JAX's collectives and lax.ppermute only.
A program may use at most 128 MiB of HBM per device.

```python
import math
import jax
import jax.numpy as jnp
from jax import lax

CX = 8
CY = 16
NZ = 512
VY = 32
VIEWS = 6
RANK = 3
KT = 15
HALF = 7
NX = 32
NY = 128
TILES = 16
N_TILE = 8


def spread_cells(values, edge, whole):
    for axis in range(3):
        values = jnp.repeat(values, edge, axis=values.ndim - 3 + axis)
    return values[..., :whole[0], :whole[1], :whole[2]]


def draw_estimate(key, part):
    edge = 8
    whole = (NX, NY, NZ)
    coarse = ((NX + edge - 1) // edge, (NY + edge - 1) // edge, (NZ + edge - 1) // edge)
    base_key, centre_key, width_key, height_key = jax.random.split(key, 4)
    background = jnp.exp(jax.random.uniform(base_key, whole, jnp.float32, math.log(0.5), math.log(2.0)))
    heights = jnp.exp(jax.random.uniform(height_key, coarse, jnp.float32, math.log(2.0), math.log(16.0)))
    centres = jax.random.uniform(centre_key, (3,) + coarse, jnp.float32, 1.5, 6.5)
    widths = jax.random.uniform(width_key, coarse, jnp.float32, 1.0, 2.5)
    centres = spread_cells(centres, edge, whole)
    widths = spread_cells(widths, edge, whole)
    heights = spread_cells(heights, edge, whole)
    distance = jnp.zeros(whole, jnp.float32)
    for axis in range(3):
        inner = (lax.broadcasted_iota(jnp.int32, whole, axis) % edge).astype(jnp.float32)
        distance = distance + (inner - centres[axis]) ** 2
    bright = heights * jnp.exp(-distance / (2.0 * widths * widths))
    return background + bright


def with_ends(array, key, least, high):
    shape = array.shape
    spot = [jax.random.randint(jax.random.fold_in(key, axis), (), 0, shape[axis]) for axis in range(len(shape))]
    array = array.at[tuple(spot)].set(least)
    longest = shape.index(max(shape))
    spot[longest] = (spot[longest] + 1) % shape[longest]
    return array.at[tuple(spot)].set(high)


def level_of(key, dims, shards, least, high):
    def one(position, shards_of):
        steps = jax.random.uniform(jax.random.fold_in(jax.random.fold_in(key, 6), position), (shards_of,), jnp.float32, least / len(shards), high / len(shards))
        return jnp.repeat(jnp.exp(steps), dims[position] // shards_of).reshape((-1,) + (1,) * (len(dims) - position - 1))

    level = one(*shards[0])
    for cut in shards[1:]:
        level = level * one(*cut)
    return level


def setup_inputs(seed: int = 0) -> dict:
    splits = jax.random.split(jax.random.key(seed), 7)
    estimate = draw_estimate(jax.random.fold_in(splits[6], 71), 0)
    observed = jnp.clip(jnp.exp(math.log(3.0) - 2.3025851 * jax.random.uniform(splits[1], (NX, TILES, VY, NZ), jnp.float32) ** level_of(splits[1], (NX, TILES, VY, NZ), ((0, 4), (1, 8)), -0.2, 0.2)), 0.3, 3.0)
    tile_offset = with_ends(jax.random.randint(splits[2], (TILES,), 0, CY * N_TILE - VY + 1), jax.random.fold_in(splits[2], 1), 0, CY * N_TILE - VY).astype(jnp.int32)
    tile_view = with_ends(jax.random.randint(splits[3], (TILES,), 0, VIEWS), jax.random.fold_in(splits[3], 1), 0, VIEWS - 1).astype(jnp.int32)
    psf_taps = jnp.clip(jnp.exp(jax.random.uniform(splits[4], (VIEWS, RANK, 3, KT), jnp.float32, math.log(0.01), math.log(0.1))), 0.01, 0.1)
    view_weight = jnp.clip(jnp.exp(jax.random.uniform(splits[5], (VIEWS,), jnp.float32, math.log(0.5), math.log(2.0))), 0.5, 2.0)
    return dict(estimate=estimate, observed=observed, tile_offset=tile_offset, tile_view=tile_view, psf_taps=psf_taps, view_weight=view_weight)


PRIOR_WEIGHT = 0.25


def taps_pass(values_in, filters, along, out_length):
    summed = filters[0] * lax.slice_in_dim(values_in, 0, out_length, axis=along)
    for k in range(1, filters.shape[0]):
        summed = summed + filters[k] * lax.slice_in_dim(values_in, k, k + out_length, axis=along)
    return summed


def reference(estimate, observed, tile_offset, tile_view, psf_taps, view_weight):
    padded = jnp.pad(estimate, HALF)
    groups_count = NX // CX

    def one_tile(carry, j):
        numerator, coverage = carry
        start_row = tile_offset[j].astype(jnp.int32)
        view_index = tile_view[j].astype(jnp.int32)
        filters = psf_taps[view_index]
        weight = view_weight[view_index]
        window = lax.dynamic_slice_in_dim(padded, start_row, VY + 2 * HALF, 1)
        blurred = jnp.zeros((NX, VY, NZ), jnp.float32)
        for q in range(RANK):
            partial_value = taps_pass(window, filters[q, 0], 0, NX)
            partial_value = taps_pass(partial_value, filters[q, 1], 1, VY)
            partial_value = taps_pass(partial_value, filters[q, 2], 2, NZ)
            blurred = blurred + partial_value
        quotient = lax.dynamic_index_in_dim(observed, j, 1, keepdims=False) / blurred
        grouped = quotient.reshape(groups_count, CX, VY, NZ)
        correction = jnp.zeros((groups_count, CX, VY, NZ), jnp.float32)
        for q in range(RANK):
            partial_value = jnp.pad(grouped, ((0, 0), (HALF, HALF), (0, 0), (0, 0)))
            partial_value = taps_pass(partial_value, filters[q, 0, ::-1], 1, CX)
            partial_value = jnp.pad(partial_value, ((0, 0), (0, 0), (HALF, HALF), (0, 0)))
            partial_value = taps_pass(partial_value, filters[q, 1, ::-1], 2, VY)
            partial_value = jnp.pad(partial_value, ((0, 0), (0, 0), (0, 0), (HALF, HALF)))
            partial_value = taps_pass(partial_value, filters[q, 2, ::-1], 3, NZ)
            correction = correction + partial_value
        correction = correction.reshape(NX, VY, NZ)
        current = lax.dynamic_slice_in_dim(numerator, start_row, VY, 1)
        numerator = lax.dynamic_update_slice_in_dim(numerator, current + weight * correction, start_row, 1)
        cover_now = lax.dynamic_slice_in_dim(coverage, start_row, VY, 0)
        coverage = lax.dynamic_update_slice_in_dim(coverage, cover_now + weight, start_row, 0)
        return (numerator, coverage), None

    start = (jnp.zeros((NX, NY, NZ), jnp.float32), jnp.zeros((NY,), jnp.float32))
    (numerator, coverage), _ = lax.scan(one_tile, start, jnp.arange(TILES, dtype=jnp.int32))
    return estimate * (numerator + PRIOR_WEIGHT) / (coverage[None, :, None] + PRIOR_WEIGHT)
```

```python
import jax
import jax.numpy as jnp
from jax import lax
from jax.sharding import PartitionSpec as P

PRIOR_WEIGHT = 0.25
MATMUL_PRECISION = lax.Precision.HIGH


def with_halo(cells, sides, width):
    for axis, dim in sides:
        count = lax.axis_size(axis)
        ends = count - 1
        head = lax.slice_in_dim(cells, 0, width, axis=dim)
        tail = lax.slice_in_dim(cells, cells.shape[dim] - width, cells.shape[dim], axis=dim)
        cells = jnp.concatenate(
            [
                lax.ppermute(tail, axis, [(i, (i + 1) % count) for i in range(ends)]),
                cells,
                lax.ppermute(head, axis, [((i + 1) % count, i) for i in range(ends)]),
            ],
            axis=dim,
        )
    return cells


def band(taps, rows, cols, shift):
    kt = taps.shape[-1]
    i = lax.broadcasted_iota(jnp.int32, (rows, cols), 0)
    j = lax.broadcasted_iota(jnp.int32, (rows, cols), 1)
    d = j - i - jnp.asarray(shift, jnp.int32)[..., None, None]
    out = jnp.zeros(d.shape[:-2] + (rows, cols), jnp.float32)
    out = jnp.broadcast_to(out, taps.shape[:-1] + (rows, cols))
    for k in range(kt):
        out = jnp.where(d == k, taps[..., k, None, None], out)
    return out


def depth_band(taps, depth, block):
    kt = taps.shape[-1]
    half = (kt - 1) // 2
    i = lax.broadcasted_iota(jnp.int32, (3 * block, block), 0)
    j = lax.broadcasted_iota(jnp.int32, (3 * block, block), 1)
    d = i - block - j + half
    strip = jnp.zeros(taps.shape[:-1] + (3 * block, block), jnp.float32)
    for k in range(kt):
        strip = jnp.where(d == k, taps[..., k, None, None], strip)
    nb = depth // block
    lead = taps.shape[:-1]
    cols = []
    for b in range(nb):
        col = jnp.pad(strip, [(0, 0)] * len(lead) + [(b * block, (nb - 1 - b) * block), (0, 0)])
        cols.append(col[..., block : block + depth, :])
    return jnp.concatenate(cols, axis=-1)


def on_device(estimate, observed, tile_offset, tile_view, psf_taps, view_weight):
    kt = psf_taps.shape[3]
    rim = (kt - 1) // 2
    block_x, block_y, depth = estimate.shape
    tile_count = observed.shape[1]
    tile_rows = observed.shape[2]
    rank_terms = psf_taps.shape[1]
    group_size = lax.axis_size("tile")
    region_rows = block_y * group_size
    win_rows = -(-(tile_rows + 2 * rim) // 8) * 8
    win_x = block_x + 2 * rim

    all_offset = lax.all_gather(tile_offset, "tile", tiled=True)
    all_view = lax.all_gather(tile_view, "tile", tiled=True)

    rimmed = with_halo(estimate, (("region", 0),), rim)
    gathered = lax.all_gather(rimmed, "tile", axis=1, tiled=True)

    filters = psf_taps[tile_view]
    weight = view_weight[tile_view]
    ax = filters[:, :, 0]
    ay = filters[:, :, 1]
    az = filters[:, :, 2]

    starts = jnp.clip(tile_offset - rim, 0, region_rows - win_rows)
    shifts = tile_offset - rim - starts
    windows = jnp.stack(
        [lax.dynamic_slice_in_dim(gathered, starts[j], win_rows, 1) for j in range(tile_count)]
    ).reshape(tile_count, win_x * win_rows, depth)

    tx = band(ax, block_x, win_x, 0)
    ty = band(ay, tile_rows, win_rows, shifts[:, None])
    kxy = (tx[:, :, :, None, :, None] * ty[:, :, None, :, None, :]).reshape(
        tile_count, rank_terms * block_x * tile_rows, win_x * win_rows
    )
    tz = depth_band(az, depth, 128)

    cells = block_x * tile_rows
    part = jnp.einsum("tmk,tkz->tmz", kxy, windows, precision=MATMUL_PRECISION)
    part = part.reshape(tile_count, rank_terms, cells, depth)
    blurred = jnp.einsum("tqmz,tqzn->tmn", part, tz, precision=MATMUL_PRECISION)

    quotient = observed.transpose(1, 0, 2, 3).reshape(tile_count, cells, depth) / blurred

    fx = band(ax[..., ::-1], block_x, block_x, -rim)
    fy = band(ay[..., ::-1], tile_rows, tile_rows, -rim)
    fxy = (fx[:, :, :, None, :, None] * fy[:, :, None, :, None, :]).reshape(
        tile_count, rank_terms * cells, cells
    )
    part = jnp.einsum("tmk,tkz->tmz", fxy, quotient, precision=MATMUL_PRECISION)
    part = part.reshape(tile_count, rank_terms, cells, depth)
    correction = jnp.einsum("tqmz,tqnz->tmn", part, tz, precision=MATMUL_PRECISION)
    weighted = (weight[:, None, None] * correction).reshape(tile_count, block_x, tile_rows, depth)

    numerator = jnp.zeros((block_x, region_rows, depth), jnp.float32)
    for j in range(tile_count):
        current = lax.dynamic_slice_in_dim(numerator, tile_offset[j], tile_rows, 1)
        numerator = lax.dynamic_update_slice_in_dim(numerator, current + weighted[j], tile_offset[j], 1)
    own_numerator = lax.psum_scatter(numerator, "tile", scatter_dimension=1, tiled=True)

    me = lax.axis_index("tile")
    rows = me * block_y + jnp.arange(block_y, dtype=jnp.int32)
    inside = (rows[None, :] >= all_offset[:, None]) & (rows[None, :] < all_offset[:, None] + tile_rows)
    own_coverage = jnp.sum(jnp.where(inside, view_weight[all_view][:, None], 0.0), axis=0)
    return estimate * (own_numerator + PRIOR_WEIGHT) / (own_coverage[None, :, None] + PRIOR_WEIGHT)


def solution(mesh):
    return jax.shard_map(
        on_device,
        mesh=mesh,
        in_specs=(
            P("region", "tile", None),
            P("region", "tile", None, None),
            P("tile"),
            P("tile"),
            P(),
            P(),
        ),
        out_specs=P("region", "tile", None),
        check_vma=False,
    )
```

```python
import jax
import jax.numpy as jnp
from jax import lax
from jax.sharding import PartitionSpec as P

PRIOR_WEIGHT = 0.25
MATMUL_PRECISION = lax.Precision.HIGH


def with_halo(cells, sides, width):
    for axis, dim in sides:
        count = lax.axis_size(axis)
        ends = count - 1
        head = lax.slice_in_dim(cells, 0, width, axis=dim)
        tail = lax.slice_in_dim(cells, cells.shape[dim] - width, cells.shape[dim], axis=dim)
        cells = jnp.concatenate(
            [
                lax.ppermute(tail, axis, [(i, (i + 1) % count) for i in range(ends)]),
                cells,
                lax.ppermute(head, axis, [((i + 1) % count, i) for i in range(ends)]),
            ],
            axis=dim,
        )
    return cells


def band(taps, rows, cols, shift):
    kt = taps.shape[-1]
    i = lax.broadcasted_iota(jnp.int32, (rows, cols), 0)
    j = lax.broadcasted_iota(jnp.int32, (rows, cols), 1)
    d = j - i - jnp.asarray(shift, jnp.int32)[..., None, None]
    out = jnp.zeros(d.shape[:-2] + (rows, cols), jnp.float32)
    out = jnp.broadcast_to(out, taps.shape[:-1] + (rows, cols))
    for k in range(kt):
        out = jnp.where(d == k, taps[..., k, None, None], out)
    return out


def kron_band(taps_a, taps_b, rows_a, rows_b, span_b, cols, shift_a, shift_b):
    kt = taps_a.shape[-1]
    lead = taps_a.shape[:-1]
    ia = lax.broadcasted_iota(jnp.int32, (rows_a, cols), 0)
    ca = lax.broadcasted_iota(jnp.int32, (rows_a, cols), 1) // span_b
    ib = lax.broadcasted_iota(jnp.int32, (rows_b, cols), 0)
    cb = lax.broadcasted_iota(jnp.int32, (rows_b, cols), 1) % span_b
    da = ca - ia - jnp.asarray(shift_a, jnp.int32)[..., None, None]
    db = cb - ib - jnp.asarray(shift_b, jnp.int32)[..., None, None]
    ea = jnp.zeros(lead + (rows_a, cols), jnp.float32)
    eb = jnp.zeros(lead + (rows_b, cols), jnp.float32)
    for k in range(kt):
        ea = jnp.where(da == k, taps_a[..., k, None, None], ea)
        eb = jnp.where(db == k, taps_b[..., k, None, None], eb)
    return ea[..., :, None, :] * eb[..., None, :, :]


def depth_band(taps, depth, block):
    kt = taps.shape[-1]
    half = (kt - 1) // 2
    i = lax.broadcasted_iota(jnp.int32, (3 * block, block), 0)
    j = lax.broadcasted_iota(jnp.int32, (3 * block, block), 1)
    d = i - block - j + half
    strip = jnp.zeros(taps.shape[:-1] + (3 * block, block), jnp.float32)
    for k in range(kt):
        strip = jnp.where(d == k, taps[..., k, None, None], strip)
    nb = depth // block
    lead = taps.shape[:-1]
    cols = []
    for b in range(nb):
        col = jnp.pad(strip, [(0, 0)] * len(lead) + [(b * block, (nb - 1 - b) * block), (0, 0)])
        cols.append(col[..., block : block + depth, :])
    return jnp.concatenate(cols, axis=-1)


def on_device(estimate, observed, tile_offset, tile_view, psf_taps, view_weight):
    kt = psf_taps.shape[3]
    rim = (kt - 1) // 2
    block_x, block_y, depth = estimate.shape
    tile_count = observed.shape[1]
    tile_rows = observed.shape[2]
    rank_terms = psf_taps.shape[1]
    group_size = lax.axis_size("tile")
    region_rows = block_y * group_size
    win_rows = -(-(tile_rows + 2 * rim) // 8) * 8
    win_x = block_x + 2 * rim

    tile_info = jnp.stack([tile_offset.astype(jnp.float32), view_weight[tile_view]], axis=1)
    all_info = lax.all_gather(tile_info, "tile", tiled=True)
    all_offset = all_info[:, 0].astype(jnp.int32)
    all_weight = all_info[:, 1]

    core = lax.all_gather(estimate, "tile", axis=1, tiled=True)
    count = lax.axis_size("region")
    lower = lax.ppermute(estimate[block_x - rim :], "region", [(i, i + 1) for i in range(count - 1)])
    upper = lax.ppermute(estimate[:rim], "region", [(i + 1, i) for i in range(count - 1)])
    rims = lax.all_gather(jnp.concatenate([lower, upper], axis=0), "tile", axis=1, tiled=True)
    gathered = jnp.concatenate([rims[:rim], core, rims[rim:]], axis=0)

    filters = psf_taps[tile_view]
    weight = view_weight[tile_view]
    ax = filters[:, :, 0]
    ay = filters[:, :, 1]
    az = filters[:, :, 2]

    starts = jnp.clip(tile_offset - rim, 0, region_rows - win_rows)
    shifts = tile_offset - rim - starts
    windows = jnp.stack(
        [lax.dynamic_slice_in_dim(gathered, starts[j], win_rows, 1) for j in range(tile_count)]
    ).reshape(tile_count, win_x * win_rows, depth)

    kxy = kron_band(ax, ay, block_x, tile_rows, win_rows, win_x * win_rows, 0, shifts[:, None]).reshape(
        tile_count, rank_terms * block_x * tile_rows, win_x * win_rows
    )
    tz = depth_band(az, depth, 128)

    cells = block_x * tile_rows
    part = jnp.einsum("tmk,tkz->tmz", kxy, windows, precision=MATMUL_PRECISION)
    part = part.reshape(tile_count, rank_terms, cells, depth)
    blurred = jnp.einsum("tqmz,tqzn->tmn", part, tz, precision=MATMUL_PRECISION)

    quotient = observed.transpose(1, 0, 2, 3).reshape(tile_count, cells, depth) / blurred

    fxy = kron_band(ax[..., ::-1], ay[..., ::-1], block_x, tile_rows, tile_rows, cells, -rim, -rim).reshape(
        tile_count, rank_terms * cells, cells
    )
    part = jnp.einsum("tmk,tkz->tmz", fxy, quotient, precision=MATMUL_PRECISION)
    part = part.reshape(tile_count, rank_terms, cells, depth)
    correction = jnp.einsum("tqmz,tqnz->tmn", part, tz, precision=MATMUL_PRECISION)
    weighted = (weight[:, None, None] * correction).reshape(tile_count, block_x, tile_rows, depth)

    numerator = jnp.zeros((block_x, region_rows, depth), jnp.float32)
    for j in range(tile_count):
        current = lax.dynamic_slice_in_dim(numerator, tile_offset[j], tile_rows, 1)
        numerator = lax.dynamic_update_slice_in_dim(numerator, current + weighted[j], tile_offset[j], 1)
    own_numerator = lax.psum_scatter(numerator, "tile", scatter_dimension=1, tiled=True)

    me = lax.axis_index("tile")
    rows = me * block_y + jnp.arange(block_y, dtype=jnp.int32)
    inside = (rows[None, :] >= all_offset[:, None]) & (rows[None, :] < all_offset[:, None] + tile_rows)
    own_coverage = jnp.sum(jnp.where(inside, all_weight[:, None], 0.0), axis=0)
    return estimate * (own_numerator + PRIOR_WEIGHT) / (own_coverage[None, :, None] + PRIOR_WEIGHT)


def solution(mesh):
    return jax.shard_map(
        on_device,
        mesh=mesh,
        in_specs=(
            P("region", "tile", None),
            P("region", "tile", None, None),
            P("tile"),
            P("tile"),
            P(),
            P(),
        ),
        out_specs=P("region", "tile", None),
        check_vma=False,
    )
```

```python
import jax
import jax.numpy as jnp
from jax import lax
from jax.sharding import PartitionSpec as P

PRIOR_WEIGHT = 0.25
MATMUL_PRECISION = lax.Precision.HIGH


def with_halo(cells, sides, width):
    for axis, dim in sides:
        count = lax.axis_size(axis)
        ends = count - 1
        head = lax.slice_in_dim(cells, 0, width, axis=dim)
        tail = lax.slice_in_dim(cells, cells.shape[dim] - width, cells.shape[dim], axis=dim)
        cells = jnp.concatenate(
            [
                lax.ppermute(tail, axis, [(i, (i + 1) % count) for i in range(ends)]),
                cells,
                lax.ppermute(head, axis, [((i + 1) % count, i) for i in range(ends)]),
            ],
            axis=dim,
        )
    return cells


def kron_band(taps_a, taps_b, rows_a, rows_b, span_b, cols, shift_a, shift_b):
    kt = taps_a.shape[-1]
    lead = taps_a.shape[:-1]
    ia = lax.broadcasted_iota(jnp.int32, (rows_a, cols), 0)
    ca = lax.broadcasted_iota(jnp.int32, (rows_a, cols), 1) // span_b
    ib = lax.broadcasted_iota(jnp.int32, (rows_b, cols), 0)
    cb = lax.broadcasted_iota(jnp.int32, (rows_b, cols), 1) % span_b
    da = ca - ia - jnp.asarray(shift_a, jnp.int32)[..., None, None]
    db = cb - ib - jnp.asarray(shift_b, jnp.int32)[..., None, None]
    ea = jnp.zeros(lead + (rows_a, cols), jnp.float32)
    eb = jnp.zeros(lead + (rows_b, cols), jnp.float32)
    for k in range(kt):
        ea = jnp.where(da == k, taps_a[..., k, None, None], ea)
        eb = jnp.where(db == k, taps_b[..., k, None, None], eb)
    return ea[..., :, None, :] * eb[..., None, :, :]


def depth_band(taps, depth, block):
    kt = taps.shape[-1]
    half = (kt - 1) // 2
    i = lax.broadcasted_iota(jnp.int32, (3 * block, block), 0)
    j = lax.broadcasted_iota(jnp.int32, (3 * block, block), 1)
    d = i - block - j + half
    strip = jnp.zeros(taps.shape[:-1] + (3 * block, block), jnp.float32)
    for k in range(kt):
        strip = jnp.where(d == k, taps[..., k, None, None], strip)
    nb = depth // block
    lead = taps.shape[:-1]
    cols = []
    for b in range(nb):
        col = jnp.pad(strip, [(0, 0)] * len(lead) + [(b * block, (nb - 1 - b) * block), (0, 0)])
        cols.append(col[..., block : block + depth, :])
    return jnp.concatenate(cols, axis=-1)


def on_device(estimate, observed, tile_offset, tile_view, psf_taps, view_weight):
    kt = psf_taps.shape[3]
    rim = (kt - 1) // 2
    block_x, block_y, depth = estimate.shape
    tile_count = observed.shape[1]
    tile_rows = observed.shape[2]
    rank_terms = psf_taps.shape[1]
    group_size = lax.axis_size("tile")
    region_rows = block_y * group_size
    win_rows = -(-(tile_rows + 2 * rim) // 8) * 8
    win_x = block_x + 2 * rim

    tile_info = jnp.stack([tile_offset.astype(jnp.float32), view_weight[tile_view]], axis=1)
    all_info = lax.all_gather(tile_info, "tile", tiled=True)
    all_offset = all_info[:, 0].astype(jnp.int32)
    all_weight = all_info[:, 1]

    rimmed = with_halo(estimate, (("region", 0),), rim)
    gathered = lax.all_gather(rimmed, "tile", axis=1, tiled=True)

    filters = psf_taps[tile_view]
    weight = view_weight[tile_view]
    ax = filters[:, :, 0]
    ay = filters[:, :, 1]
    az = filters[:, :, 2]

    starts = jnp.clip(tile_offset - rim, 0, region_rows - win_rows)
    shifts = tile_offset - rim - starts
    windows = jnp.stack(
        [lax.dynamic_slice_in_dim(gathered, starts[j], win_rows, 1) for j in range(tile_count)]
    ).reshape(tile_count, win_x * win_rows, depth)

    kxy = kron_band(ax, ay, block_x, tile_rows, win_rows, win_x * win_rows, 0, shifts[:, None]).reshape(
        tile_count, rank_terms * block_x * tile_rows, win_x * win_rows
    )
    tz = depth_band(az, depth, 128)

    cells = block_x * tile_rows
    part = jnp.einsum("tmk,tkz->tmz", kxy, windows, precision=MATMUL_PRECISION)
    part = part.reshape(tile_count, rank_terms, cells, depth)
    blurred = jnp.einsum("tqmz,tqzn->tmn", part, tz, precision=MATMUL_PRECISION)

    quotient = observed.transpose(1, 0, 2, 3).reshape(tile_count, cells, depth) / blurred

    fxy = kron_band(ax[..., ::-1], ay[..., ::-1], block_x, tile_rows, tile_rows, cells, -rim, -rim).reshape(
        tile_count, rank_terms * cells, cells
    )
    part = jnp.einsum("tmk,tkz->tmz", fxy, quotient, precision=MATMUL_PRECISION)
    part = part.reshape(tile_count, rank_terms, cells, depth)
    correction = jnp.einsum("tqmz,tqnz->tmn", part, tz, precision=MATMUL_PRECISION)
    weighted = (weight[:, None, None] * correction).reshape(tile_count, block_x, tile_rows, depth)

    numerator = jnp.zeros((block_x, region_rows, depth), jnp.float32)
    for j in range(tile_count):
        current = lax.dynamic_slice_in_dim(numerator, tile_offset[j], tile_rows, 1)
        numerator = lax.dynamic_update_slice_in_dim(numerator, current + weighted[j], tile_offset[j], 1)
    own_numerator = lax.psum_scatter(numerator, "tile", scatter_dimension=1, tiled=True)

    me = lax.axis_index("tile")
    rows = me * block_y + jnp.arange(block_y, dtype=jnp.int32)
    inside = (rows[None, :] >= all_offset[:, None]) & (rows[None, :] < all_offset[:, None] + tile_rows)
    own_coverage = jnp.sum(jnp.where(inside, all_weight[:, None], 0.0), axis=0)
    return estimate * (own_numerator + PRIOR_WEIGHT) / (own_coverage[None, :, None] + PRIOR_WEIGHT)


def solution(mesh):
    return jax.shard_map(
        on_device,
        mesh=mesh,
        in_specs=(
            P("region", "tile", None),
            P("region", "tile", None, None),
            P("tile"),
            P("tile"),
            P(),
            P(),
        ),
        out_specs=P("region", "tile", None),
        check_vma=False,
    )
```

```python
import jax
import jax.numpy as jnp
from jax import lax
from jax.sharding import PartitionSpec as P

PRIOR_WEIGHT = 0.25
MATMUL_PRECISION = lax.Precision.HIGH


def with_halo(cells, sides, width):
    for axis, dim in sides:
        count = lax.axis_size(axis)
        ends = count - 1
        head = lax.slice_in_dim(cells, 0, width, axis=dim)
        tail = lax.slice_in_dim(cells, cells.shape[dim] - width, cells.shape[dim], axis=dim)
        cells = jnp.concatenate(
            [
                lax.ppermute(tail, axis, [(i, (i + 1) % count) for i in range(ends)]),
                cells,
                lax.ppermute(head, axis, [((i + 1) % count, i) for i in range(ends)]),
            ],
            axis=dim,
        )
    return cells


def kron_band(taps_a, taps_b, rows_a, rows_b, span_b, cols, shift_a, shift_b):
    kt = taps_a.shape[-1]
    lead = taps_a.shape[:-1]
    ia = lax.broadcasted_iota(jnp.int32, (rows_a, cols), 0)
    ca = lax.broadcasted_iota(jnp.int32, (rows_a, cols), 1) // span_b
    ib = lax.broadcasted_iota(jnp.int32, (rows_b, cols), 0)
    cb = lax.broadcasted_iota(jnp.int32, (rows_b, cols), 1) % span_b
    da = ca - ia - jnp.asarray(shift_a, jnp.int32)[..., None, None]
    db = cb - ib - jnp.asarray(shift_b, jnp.int32)[..., None, None]
    ea = jnp.zeros(lead + (rows_a, cols), jnp.float32)
    eb = jnp.zeros(lead + (rows_b, cols), jnp.float32)
    for k in range(kt):
        ea = jnp.where(da == k, taps_a[..., k, None, None], ea)
        eb = jnp.where(db == k, taps_b[..., k, None, None], eb)
    return ea[..., :, None, :] * eb[..., None, :, :]


def depth_band(taps, depth, block):
    kt = taps.shape[-1]
    half = (kt - 1) // 2
    i = lax.broadcasted_iota(jnp.int32, (3 * block, block), 0)
    j = lax.broadcasted_iota(jnp.int32, (3 * block, block), 1)
    d = i - block - j + half
    strip = jnp.zeros(taps.shape[:-1] + (3 * block, block), jnp.float32)
    for k in range(kt):
        strip = jnp.where(d == k, taps[..., k, None, None], strip)
    nb = depth // block
    lead = taps.shape[:-1]
    cols = []
    for b in range(nb):
        col = jnp.pad(strip, [(0, 0)] * len(lead) + [(b * block, (nb - 1 - b) * block), (0, 0)])
        cols.append(col[..., block : block + depth, :])
    return jnp.concatenate(cols, axis=-1)


def on_device(estimate, observed, tile_offset, tile_view, psf_taps, view_weight):
    kt = psf_taps.shape[3]
    rim = (kt - 1) // 2
    block_x, block_y, depth = estimate.shape
    tile_count = observed.shape[1]
    tile_rows = observed.shape[2]
    rank_terms = psf_taps.shape[1]
    group_size = lax.axis_size("tile")
    region_rows = block_y * group_size
    win_rows = -(-(tile_rows + 2 * rim) // 8) * 8
    win_x = block_x + 2 * rim

    tile_info = jnp.stack([tile_offset.astype(jnp.float32), view_weight[tile_view]], axis=1)
    all_info = lax.all_gather(tile_info, "tile", tiled=True)
    all_offset = all_info[:, 0].astype(jnp.int32)
    all_weight = all_info[:, 1]

    core = lax.all_gather(estimate, "tile", axis=1, tiled=True)
    count = lax.axis_size("region")
    half_rows = region_rows // 2
    side = lax.axis_index("tile") % 2
    mine = side * half_rows
    lower = lax.ppermute(
        lax.dynamic_slice_in_dim(core[block_x - rim :], mine, half_rows, 1),
        "region", [(i, i + 1) for i in range(count - 1)],
    )
    upper = lax.ppermute(
        lax.dynamic_slice_in_dim(core[:rim], mine, half_rows, 1),
        "region", [(i + 1, i) for i in range(count - 1)],
    )
    fetched = jnp.concatenate([lower, upper], axis=0)
    swapped = lax.ppermute(
        fetched, "tile", [(i, i ^ 1) for i in range(group_size)]
    )
    rims = jnp.where(side == 0, jnp.concatenate([fetched, swapped], axis=1), jnp.concatenate([swapped, fetched], axis=1))
    gathered = jnp.concatenate([rims[:rim], core, rims[rim:]], axis=0)

    filters = psf_taps[tile_view]
    weight = view_weight[tile_view]
    ax = filters[:, :, 0]
    ay = filters[:, :, 1]
    az = filters[:, :, 2]

    starts = jnp.clip(tile_offset - rim, 0, region_rows - win_rows)
    shifts = tile_offset - rim - starts
    windows = jnp.stack(
        [lax.dynamic_slice_in_dim(gathered, starts[j], win_rows, 1) for j in range(tile_count)]
    ).reshape(tile_count, win_x * win_rows, depth)

    kxy = kron_band(ax, ay, block_x, tile_rows, win_rows, win_x * win_rows, 0, shifts[:, None]).reshape(
        tile_count, rank_terms * block_x * tile_rows, win_x * win_rows
    )
    tz = depth_band(az, depth, 128)

    cells = block_x * tile_rows
    part = jnp.einsum("tmk,tkz->tmz", kxy, windows, precision=MATMUL_PRECISION)
    part = part.reshape(tile_count, rank_terms, cells, depth)
    blurred = jnp.einsum("tqmz,tqzn->tmn", part, tz, precision=MATMUL_PRECISION)

    quotient = observed.transpose(1, 0, 2, 3).reshape(tile_count, cells, depth) / blurred

    fxy = kron_band(ax[..., ::-1], ay[..., ::-1], block_x, tile_rows, tile_rows, cells, -rim, -rim).reshape(
        tile_count, rank_terms * cells, cells
    )
    part = jnp.einsum("tmk,tkz->tmz", fxy, quotient, precision=MATMUL_PRECISION)
    part = part.reshape(tile_count, rank_terms, cells, depth)
    correction = jnp.einsum("tqmz,tqnz->tmn", part, tz, precision=MATMUL_PRECISION)
    weighted = (weight[:, None, None] * correction).reshape(tile_count, block_x, tile_rows, depth)

    numerator = jnp.zeros((block_x, region_rows, depth), jnp.float32)
    for j in range(tile_count):
        current = lax.dynamic_slice_in_dim(numerator, tile_offset[j], tile_rows, 1)
        numerator = lax.dynamic_update_slice_in_dim(numerator, current + weighted[j], tile_offset[j], 1)
    own_numerator = lax.psum_scatter(numerator, "tile", scatter_dimension=1, tiled=True)

    me = lax.axis_index("tile")
    rows = me * block_y + jnp.arange(block_y, dtype=jnp.int32)
    inside = (rows[None, :] >= all_offset[:, None]) & (rows[None, :] < all_offset[:, None] + tile_rows)
    own_coverage = jnp.sum(jnp.where(inside, all_weight[:, None], 0.0), axis=0)
    return estimate * (own_numerator + PRIOR_WEIGHT) / (own_coverage[None, :, None] + PRIOR_WEIGHT)


def solution(mesh):
    return jax.shard_map(
        on_device,
        mesh=mesh,
        in_specs=(
            P("region", "tile", None),
            P("region", "tile", None, None),
            P("tile"),
            P("tile"),
            P(),
            P(),
        ),
        out_specs=P("region", "tile", None),
        check_vma=False,
    )
```

```python
import jax
import jax.numpy as jnp
from jax import lax
from jax.sharding import PartitionSpec as P

PRIOR_WEIGHT = 0.25
MATMUL_PRECISION = lax.Precision.HIGH


def with_halo(cells, sides, width):
    for axis, dim in sides:
        count = lax.axis_size(axis)
        ends = count - 1
        head = lax.slice_in_dim(cells, 0, width, axis=dim)
        tail = lax.slice_in_dim(cells, cells.shape[dim] - width, cells.shape[dim], axis=dim)
        cells = jnp.concatenate(
            [
                lax.ppermute(tail, axis, [(i, (i + 1) % count) for i in range(ends)]),
                cells,
                lax.ppermute(head, axis, [((i + 1) % count, i) for i in range(ends)]),
            ],
            axis=dim,
        )
    return cells


def kron_band(taps_a, taps_b, rows_a, rows_b, span_b, cols, shift_a, shift_b):
    kt = taps_a.shape[-1]
    lead = taps_a.shape[:-1]
    ia = lax.broadcasted_iota(jnp.int32, (rows_a, cols), 0)
    ca = lax.broadcasted_iota(jnp.int32, (rows_a, cols), 1) // span_b
    ib = lax.broadcasted_iota(jnp.int32, (rows_b, cols), 0)
    cb = lax.broadcasted_iota(jnp.int32, (rows_b, cols), 1) % span_b
    da = ca - ia - jnp.asarray(shift_a, jnp.int32)[..., None, None]
    db = cb - ib - jnp.asarray(shift_b, jnp.int32)[..., None, None]
    ea = jnp.zeros(lead + (rows_a, cols), jnp.float32)
    eb = jnp.zeros(lead + (rows_b, cols), jnp.float32)
    for k in range(kt):
        ea = jnp.where(da == k, taps_a[..., k, None, None], ea)
        eb = jnp.where(db == k, taps_b[..., k, None, None], eb)
    return ea[..., :, None, :] * eb[..., None, :, :]


def depth_band(taps, depth, block):
    kt = taps.shape[-1]
    half = (kt - 1) // 2
    i = lax.broadcasted_iota(jnp.int32, (3 * block, block), 0)
    j = lax.broadcasted_iota(jnp.int32, (3 * block, block), 1)
    d = i - block - j + half
    strip = jnp.zeros(taps.shape[:-1] + (3 * block, block), jnp.float32)
    for k in range(kt):
        strip = jnp.where(d == k, taps[..., k, None, None], strip)
    nb = depth // block
    lead = taps.shape[:-1]
    cols = []
    for b in range(nb):
        col = jnp.pad(strip, [(0, 0)] * len(lead) + [(b * block, (nb - 1 - b) * block), (0, 0)])
        cols.append(col[..., block : block + depth, :])
    return jnp.concatenate(cols, axis=-1)


def on_device(estimate, observed, tile_offset, tile_view, psf_taps, view_weight):
    kt = psf_taps.shape[3]
    rim = (kt - 1) // 2
    block_x, block_y, depth = estimate.shape
    tile_count = observed.shape[1]
    tile_rows = observed.shape[2]
    rank_terms = psf_taps.shape[1]
    group_size = lax.axis_size("tile")
    region_rows = block_y * group_size
    win_rows = -(-(tile_rows + 2 * rim) // 8) * 8
    win_x = block_x + 2 * rim

    tile_info = jnp.stack([tile_offset.astype(jnp.float32), view_weight[tile_view]], axis=1)
    all_info = lax.all_gather(tile_info, "tile", tiled=True)
    all_offset = all_info[:, 0].astype(jnp.int32)
    all_weight = all_info[:, 1]

    rimmed = with_halo(estimate, (("region", 0),), rim)
    gathered = lax.all_gather(rimmed, "tile", axis=1, tiled=True)

    filters = psf_taps[tile_view]
    weight = view_weight[tile_view]
    ax = filters[:, :, 0]
    ay = filters[:, :, 1]
    az = filters[:, :, 2]

    starts = jnp.clip(tile_offset - rim, 0, region_rows - win_rows)
    shifts = tile_offset - rim - starts

    kxy = kron_band(ax, ay, block_x, tile_rows, win_rows, win_x * win_rows, 0, shifts[:, None]).reshape(
        tile_count, rank_terms * block_x * tile_rows, win_x * win_rows
    )
    fxy = kron_band(ax[..., ::-1], ay[..., ::-1], block_x, tile_rows, tile_rows, block_x * tile_rows, -rim, -rim)
    tz = depth_band(az, depth, 128)

    cells = block_x * tile_rows
    fxy = fxy.reshape(tile_count, rank_terms * cells, cells)
    obs = observed.transpose(1, 0, 2, 3).reshape(tile_count, cells, depth)

    out_block = 256 if depth % 256 == 0 else depth
    reach = 128

    def along_depth(part, mats, flipped):
        pieces = []
        for b in range(depth // out_block):
            lo = max(b * out_block - reach, 0)
            hi = min((b + 1) * out_block + reach, depth)
            cols = slice(b * out_block, (b + 1) * out_block)
            if flipped:
                m = mats[:, cols, lo:hi]
                pieces.append(jnp.einsum("qmz,qnz->mn", part[:, :, lo:hi], m, precision=MATMUL_PRECISION))
            else:
                m = mats[:, lo:hi, cols]
                pieces.append(jnp.einsum("qmz,qzn->mn", part[:, :, lo:hi], m, precision=MATMUL_PRECISION))
        return jnp.concatenate(pieces, axis=-1)

    weighted = []
    for j in range(tile_count):
        window = lax.dynamic_slice_in_dim(gathered, starts[j], win_rows, 1).reshape(win_x * win_rows, depth)
        part = jnp.dot(kxy[j], window, precision=MATMUL_PRECISION).reshape(rank_terms, cells, depth)
        blurred = along_depth(part, tz[j], False)
        quotient = obs[j] / blurred
        part = jnp.dot(fxy[j], quotient, precision=MATMUL_PRECISION).reshape(rank_terms, cells, depth)
        correction = along_depth(part, tz[j], True)
        weighted.append((weight[j] * correction).reshape(block_x, tile_rows, depth))

    numerator = jnp.zeros((block_x, region_rows, depth), jnp.float32)
    for j in range(tile_count):
        current = lax.dynamic_slice_in_dim(numerator, tile_offset[j], tile_rows, 1)
        numerator = lax.dynamic_update_slice_in_dim(numerator, current + weighted[j], tile_offset[j], 1)
    own_numerator = lax.psum_scatter(numerator, "tile", scatter_dimension=1, tiled=True)

    me = lax.axis_index("tile")
    rows = me * block_y + jnp.arange(block_y, dtype=jnp.int32)
    inside = (rows[None, :] >= all_offset[:, None]) & (rows[None, :] < all_offset[:, None] + tile_rows)
    own_coverage = jnp.sum(jnp.where(inside, all_weight[:, None], 0.0), axis=0)
    return estimate * (own_numerator + PRIOR_WEIGHT) / (own_coverage[None, :, None] + PRIOR_WEIGHT)


def solution(mesh):
    return jax.shard_map(
        on_device,
        mesh=mesh,
        in_specs=(
            P("region", "tile", None),
            P("region", "tile", None, None),
            P("tile"),
            P("tile"),
            P(),
            P(),
        ),
        out_specs=P("region", "tile", None),
        check_vma=False,
    )
```

```python
import jax
import jax.numpy as jnp
from jax import lax
from jax.sharding import PartitionSpec as P

PRIOR_WEIGHT = 0.25
MATMUL_PRECISION = lax.Precision.HIGH


def with_halo(cells, sides, width):
    for axis, dim in sides:
        count = lax.axis_size(axis)
        ends = count - 1
        head = lax.slice_in_dim(cells, 0, width, axis=dim)
        tail = lax.slice_in_dim(cells, cells.shape[dim] - width, cells.shape[dim], axis=dim)
        cells = jnp.concatenate(
            [
                lax.ppermute(tail, axis, [(i, (i + 1) % count) for i in range(ends)]),
                cells,
                lax.ppermute(head, axis, [((i + 1) % count, i) for i in range(ends)]),
            ],
            axis=dim,
        )
    return cells


def split_bf16(values):
    high = values.astype(jnp.bfloat16)
    return high, (values - high.astype(jnp.float32)).astype(jnp.bfloat16)


def dot_rounded_data(spec, data, taps, data_first):
    data_high = data.astype(jnp.bfloat16)
    taps_high, taps_low = split_bf16(taps)
    if data_first:
        terms = [(data_high, taps_high), (data_high, taps_low)]
    else:
        terms = [(taps_high, data_high), (taps_low, data_high)]
    return sum(jnp.einsum(spec, a, b, preferred_element_type=jnp.float32) for a, b in terms)


def kron_band(taps_a, taps_b, rows_a, rows_b, span_b, cols, shift_a, shift_b):
    kt = taps_a.shape[-1]
    lead = taps_a.shape[:-1]
    ia = lax.broadcasted_iota(jnp.int32, (rows_a, cols), 0)
    ca = lax.broadcasted_iota(jnp.int32, (rows_a, cols), 1) // span_b
    ib = lax.broadcasted_iota(jnp.int32, (rows_b, cols), 0)
    cb = lax.broadcasted_iota(jnp.int32, (rows_b, cols), 1) % span_b
    da = ca - ia - jnp.asarray(shift_a, jnp.int32)[..., None, None]
    db = cb - ib - jnp.asarray(shift_b, jnp.int32)[..., None, None]
    ea = jnp.zeros(lead + (rows_a, cols), jnp.float32)
    eb = jnp.zeros(lead + (rows_b, cols), jnp.float32)
    for k in range(kt):
        ea = jnp.where(da == k, taps_a[..., k, None, None], ea)
        eb = jnp.where(db == k, taps_b[..., k, None, None], eb)
    return ea[..., :, None, :] * eb[..., None, :, :]


def depth_band(taps, depth, block):
    kt = taps.shape[-1]
    half = (kt - 1) // 2
    i = lax.broadcasted_iota(jnp.int32, (3 * block, block), 0)
    j = lax.broadcasted_iota(jnp.int32, (3 * block, block), 1)
    d = i - block - j + half
    strip = jnp.zeros(taps.shape[:-1] + (3 * block, block), jnp.float32)
    for k in range(kt):
        strip = jnp.where(d == k, taps[..., k, None, None], strip)
    nb = depth // block
    lead = taps.shape[:-1]
    cols = []
    for b in range(nb):
        col = jnp.pad(strip, [(0, 0)] * len(lead) + [(b * block, (nb - 1 - b) * block), (0, 0)])
        cols.append(col[..., block : block + depth, :])
    return jnp.concatenate(cols, axis=-1)


def on_device(estimate, observed, tile_offset, tile_view, psf_taps, view_weight):
    kt = psf_taps.shape[3]
    rim = (kt - 1) // 2
    block_x, block_y, depth = estimate.shape
    tile_count = observed.shape[1]
    tile_rows = observed.shape[2]
    rank_terms = psf_taps.shape[1]
    group_size = lax.axis_size("tile")
    region_rows = block_y * group_size
    win_rows = -(-(tile_rows + 2 * rim) // 8) * 8
    win_x = block_x + 2 * rim

    tile_info = jnp.stack([tile_offset.astype(jnp.float32), view_weight[tile_view]], axis=1)
    all_info = lax.all_gather(tile_info, "tile", tiled=True)
    all_offset = all_info[:, 0].astype(jnp.int32)
    all_weight = all_info[:, 1]

    rimmed = with_halo(estimate, (("region", 0),), rim)
    gathered = lax.all_gather(rimmed, "tile", axis=1, tiled=True)

    filters = psf_taps[tile_view]
    weight = view_weight[tile_view]
    ax = filters[:, :, 0]
    ay = filters[:, :, 1]
    az = filters[:, :, 2]

    starts = jnp.clip(tile_offset - rim, 0, region_rows - win_rows)
    shifts = tile_offset - rim - starts
    windows = jnp.stack(
        [lax.dynamic_slice_in_dim(gathered, starts[j], win_rows, 1) for j in range(tile_count)]
    ).reshape(tile_count, win_x * win_rows, depth)

    kxy = kron_band(ax, ay, block_x, tile_rows, win_rows, win_x * win_rows, 0, shifts[:, None]).reshape(
        tile_count, rank_terms * block_x * tile_rows, win_x * win_rows
    )
    tz = depth_band(az, depth, 128)

    cells = block_x * tile_rows
    part = jnp.einsum("tmk,tkz->tmz", kxy, windows, precision=MATMUL_PRECISION)
    part = part.reshape(tile_count, rank_terms, cells, depth)
    blurred = dot_rounded_data("tqmz,tqzn->tmn", part, tz, True)

    quotient = observed.transpose(1, 0, 2, 3).reshape(tile_count, cells, depth) / blurred

    fxy = kron_band(ax[..., ::-1], ay[..., ::-1], block_x, tile_rows, tile_rows, cells, -rim, -rim).reshape(
        tile_count, rank_terms * cells, cells
    )
    part = dot_rounded_data("tmk,tkz->tmz", quotient, fxy, False)
    part = part.reshape(tile_count, rank_terms, cells, depth)
    correction = jnp.einsum("tqmz,tqnz->tmn", part, tz, precision=MATMUL_PRECISION)
    weighted = (weight[:, None, None] * correction).reshape(tile_count, block_x, tile_rows, depth)

    numerator = jnp.zeros((block_x, region_rows, depth), jnp.float32)
    for j in range(tile_count):
        current = lax.dynamic_slice_in_dim(numerator, tile_offset[j], tile_rows, 1)
        numerator = lax.dynamic_update_slice_in_dim(numerator, current + weighted[j], tile_offset[j], 1)
    own_numerator = lax.psum_scatter(numerator, "tile", scatter_dimension=1, tiled=True)

    me = lax.axis_index("tile")
    rows = me * block_y + jnp.arange(block_y, dtype=jnp.int32)
    inside = (rows[None, :] >= all_offset[:, None]) & (rows[None, :] < all_offset[:, None] + tile_rows)
    own_coverage = jnp.sum(jnp.where(inside, all_weight[:, None], 0.0), axis=0)
    return estimate * (own_numerator + PRIOR_WEIGHT) / (own_coverage[None, :, None] + PRIOR_WEIGHT)


def solution(mesh):
    return jax.shard_map(
        on_device,
        mesh=mesh,
        in_specs=(
            P("region", "tile", None),
            P("region", "tile", None, None),
            P("tile"),
            P("tile"),
            P(),
            P(),
        ),
        out_specs=P("region", "tile", None),
        check_vma=False,
    )
```

```python
import jax
import jax.numpy as jnp
from jax import lax
from jax.sharding import PartitionSpec as P

PRIOR_WEIGHT = 0.25
MATMUL_PRECISION = lax.Precision.HIGH


def with_halo(cells, sides, width):
    for axis, dim in sides:
        count = lax.axis_size(axis)
        ends = count - 1
        head = lax.slice_in_dim(cells, 0, width, axis=dim)
        tail = lax.slice_in_dim(cells, cells.shape[dim] - width, cells.shape[dim], axis=dim)
        cells = jnp.concatenate(
            [
                lax.ppermute(tail, axis, [(i, (i + 1) % count) for i in range(ends)]),
                cells,
                lax.ppermute(head, axis, [((i + 1) % count, i) for i in range(ends)]),
            ],
            axis=dim,
        )
    return cells


def split_bf16(values):
    high = lax.reduce_precision(values, exponent_bits=8, mantissa_bits=7)
    return high.astype(jnp.bfloat16), (values - high).astype(jnp.bfloat16)


def dot_rounded_data(spec, data, taps, data_first):
    data_high = data.astype(jnp.bfloat16)
    taps_high, taps_low = split_bf16(taps)
    if data_first:
        terms = [(data_high, taps_high), (data_high, taps_low)]
    else:
        terms = [(taps_high, data_high), (taps_low, data_high)]
    return sum(jnp.einsum(spec, a, b, preferred_element_type=jnp.float32) for a, b in terms)


def kron_band(taps_a, taps_b, rows_a, rows_b, span_b, cols, shift_a, shift_b):
    kt = taps_a.shape[-1]
    lead = taps_a.shape[:-1]
    ia = lax.broadcasted_iota(jnp.int32, (rows_a, cols), 0)
    ca = lax.broadcasted_iota(jnp.int32, (rows_a, cols), 1) // span_b
    ib = lax.broadcasted_iota(jnp.int32, (rows_b, cols), 0)
    cb = lax.broadcasted_iota(jnp.int32, (rows_b, cols), 1) % span_b
    da = ca - ia - jnp.asarray(shift_a, jnp.int32)[..., None, None]
    db = cb - ib - jnp.asarray(shift_b, jnp.int32)[..., None, None]
    ea = jnp.zeros(lead + (rows_a, cols), jnp.float32)
    eb = jnp.zeros(lead + (rows_b, cols), jnp.float32)
    for k in range(kt):
        ea = jnp.where(da == k, taps_a[..., k, None, None], ea)
        eb = jnp.where(db == k, taps_b[..., k, None, None], eb)
    return ea[..., :, None, :] * eb[..., None, :, :]


def depth_band(taps, depth, block):
    kt = taps.shape[-1]
    half = (kt - 1) // 2
    i = lax.broadcasted_iota(jnp.int32, (3 * block, block), 0)
    j = lax.broadcasted_iota(jnp.int32, (3 * block, block), 1)
    d = i - block - j + half
    strip = jnp.zeros(taps.shape[:-1] + (3 * block, block), jnp.float32)
    for k in range(kt):
        strip = jnp.where(d == k, taps[..., k, None, None], strip)
    nb = depth // block
    lead = taps.shape[:-1]
    cols = []
    for b in range(nb):
        col = jnp.pad(strip, [(0, 0)] * len(lead) + [(b * block, (nb - 1 - b) * block), (0, 0)])
        cols.append(col[..., block : block + depth, :])
    return jnp.concatenate(cols, axis=-1)


def on_device(estimate, observed, tile_offset, tile_view, psf_taps, view_weight):
    kt = psf_taps.shape[3]
    rim = (kt - 1) // 2
    block_x, block_y, depth = estimate.shape
    tile_count = observed.shape[1]
    tile_rows = observed.shape[2]
    rank_terms = psf_taps.shape[1]
    group_size = lax.axis_size("tile")
    region_rows = block_y * group_size
    win_rows = -(-(tile_rows + 2 * rim) // 8) * 8
    win_x = block_x + 2 * rim

    tile_info = jnp.stack([tile_offset.astype(jnp.float32), view_weight[tile_view]], axis=1)
    all_info = lax.all_gather(tile_info, "tile", tiled=True)
    all_offset = all_info[:, 0].astype(jnp.int32)
    all_weight = all_info[:, 1]

    rimmed = with_halo(estimate, (("region", 0),), rim)
    gathered = lax.all_gather(rimmed, "tile", axis=1, tiled=True)

    filters = psf_taps[tile_view]
    weight = view_weight[tile_view]
    ax = filters[:, :, 0]
    ay = filters[:, :, 1]
    az = filters[:, :, 2]

    starts = jnp.clip(tile_offset - rim, 0, region_rows - win_rows)
    shifts = tile_offset - rim - starts
    windows = jnp.stack(
        [lax.dynamic_slice_in_dim(gathered, starts[j], win_rows, 1) for j in range(tile_count)]
    ).reshape(tile_count, win_x * win_rows, depth)

    kxy = kron_band(ax, ay, block_x, tile_rows, win_rows, win_x * win_rows, 0, shifts[:, None]).reshape(
        tile_count, rank_terms * block_x * tile_rows, win_x * win_rows
    )
    tz = depth_band(az, depth, 128)

    cells = block_x * tile_rows
    part = jnp.einsum("tmk,tkz->tmz", kxy, windows, precision=MATMUL_PRECISION)
    part = part.reshape(tile_count, rank_terms, cells, depth)
    blurred = dot_rounded_data("tqmz,tqzn->tmn", part, tz, True)

    quotient = observed.transpose(1, 0, 2, 3).reshape(tile_count, cells, depth) / blurred

    fxy = kron_band(ax[..., ::-1], ay[..., ::-1], block_x, tile_rows, tile_rows, cells, -rim, -rim).reshape(
        tile_count, rank_terms * cells, cells
    )
    part = dot_rounded_data("tmk,tkz->tmz", quotient, fxy, False)
    part = part.reshape(tile_count, rank_terms, cells, depth)
    correction = jnp.einsum("tqmz,tqnz->tmn", part, tz, precision=MATMUL_PRECISION)
    weighted = (weight[:, None, None] * correction).reshape(tile_count, block_x, tile_rows, depth)

    numerator = jnp.zeros((block_x, region_rows, depth), jnp.float32)
    for j in range(tile_count):
        current = lax.dynamic_slice_in_dim(numerator, tile_offset[j], tile_rows, 1)
        numerator = lax.dynamic_update_slice_in_dim(numerator, current + weighted[j], tile_offset[j], 1)
    own_numerator = lax.psum_scatter(numerator, "tile", scatter_dimension=1, tiled=True)

    me = lax.axis_index("tile")
    rows = me * block_y + jnp.arange(block_y, dtype=jnp.int32)
    inside = (rows[None, :] >= all_offset[:, None]) & (rows[None, :] < all_offset[:, None] + tile_rows)
    own_coverage = jnp.sum(jnp.where(inside, all_weight[:, None], 0.0), axis=0)
    return estimate * (own_numerator + PRIOR_WEIGHT) / (own_coverage[None, :, None] + PRIOR_WEIGHT)


def solution(mesh):
    return jax.shard_map(
        on_device,
        mesh=mesh,
        in_specs=(
            P("region", "tile", None),
            P("region", "tile", None, None),
            P("tile"),
            P("tile"),
            P(),
            P(),
        ),
        out_specs=P("region", "tile", None),
        check_vma=False,
    )
```

```python
import jax
import jax.numpy as jnp
from jax import lax
from jax.sharding import PartitionSpec as P

PRIOR_WEIGHT = 0.25
MATMUL_PRECISION = lax.Precision.HIGH


def with_halo(cells, sides, width):
    for axis, dim in sides:
        count = lax.axis_size(axis)
        ends = count - 1
        head = lax.slice_in_dim(cells, 0, width, axis=dim)
        tail = lax.slice_in_dim(cells, cells.shape[dim] - width, cells.shape[dim], axis=dim)
        cells = jnp.concatenate(
            [
                lax.ppermute(tail, axis, [(i, (i + 1) % count) for i in range(ends)]),
                cells,
                lax.ppermute(head, axis, [((i + 1) % count, i) for i in range(ends)]),
            ],
            axis=dim,
        )
    return cells


def split_bf16(values):
    high = lax.reduce_precision(values, exponent_bits=8, mantissa_bits=7)
    return high.astype(jnp.bfloat16), (values - high).astype(jnp.bfloat16)


def dot_rounded_data(spec, data, taps, data_first):
    data_high = lax.reduce_precision(data, exponent_bits=8, mantissa_bits=7).astype(jnp.bfloat16)
    taps_high, taps_low = split_bf16(taps)
    if data_first:
        terms = [(data_high, taps_high), (data_high, taps_low)]
    else:
        terms = [(taps_high, data_high), (taps_low, data_high)]
    return sum(jnp.einsum(spec, a, b, preferred_element_type=jnp.float32) for a, b in terms)


def kron_band(taps_a, taps_b, rows_a, rows_b, span_b, cols, shift_a, shift_b):
    kt = taps_a.shape[-1]
    lead = taps_a.shape[:-1]
    ia = lax.broadcasted_iota(jnp.int32, (rows_a, cols), 0)
    ca = lax.broadcasted_iota(jnp.int32, (rows_a, cols), 1) // span_b
    ib = lax.broadcasted_iota(jnp.int32, (rows_b, cols), 0)
    cb = lax.broadcasted_iota(jnp.int32, (rows_b, cols), 1) % span_b
    da = ca - ia - jnp.asarray(shift_a, jnp.int32)[..., None, None]
    db = cb - ib - jnp.asarray(shift_b, jnp.int32)[..., None, None]
    ea = jnp.zeros(lead + (rows_a, cols), jnp.float32)
    eb = jnp.zeros(lead + (rows_b, cols), jnp.float32)
    for k in range(kt):
        ea = jnp.where(da == k, taps_a[..., k, None, None], ea)
        eb = jnp.where(db == k, taps_b[..., k, None, None], eb)
    return ea[..., :, None, :] * eb[..., None, :, :]


def depth_band(taps, depth, block):
    kt = taps.shape[-1]
    half = (kt - 1) // 2
    i = lax.broadcasted_iota(jnp.int32, (3 * block, block), 0)
    j = lax.broadcasted_iota(jnp.int32, (3 * block, block), 1)
    d = i - block - j + half
    strip = jnp.zeros(taps.shape[:-1] + (3 * block, block), jnp.float32)
    for k in range(kt):
        strip = jnp.where(d == k, taps[..., k, None, None], strip)
    nb = depth // block
    lead = taps.shape[:-1]
    cols = []
    for b in range(nb):
        col = jnp.pad(strip, [(0, 0)] * len(lead) + [(b * block, (nb - 1 - b) * block), (0, 0)])
        cols.append(col[..., block : block + depth, :])
    return jnp.concatenate(cols, axis=-1)


def on_device(estimate, observed, tile_offset, tile_view, psf_taps, view_weight):
    kt = psf_taps.shape[3]
    rim = (kt - 1) // 2
    block_x, block_y, depth = estimate.shape
    tile_count = observed.shape[1]
    tile_rows = observed.shape[2]
    rank_terms = psf_taps.shape[1]
    group_size = lax.axis_size("tile")
    region_rows = block_y * group_size
    win_rows = -(-(tile_rows + 2 * rim) // 8) * 8
    win_x = block_x + 2 * rim

    tile_info = jnp.stack([tile_offset.astype(jnp.float32), view_weight[tile_view]], axis=1)
    all_info = lax.all_gather(tile_info, "tile", tiled=True)
    all_offset = all_info[:, 0].astype(jnp.int32)
    all_weight = all_info[:, 1]

    rimmed = with_halo(estimate, (("region", 0),), rim)
    gathered = lax.all_gather(rimmed, "tile", axis=1, tiled=True)

    filters = psf_taps[tile_view]
    weight = view_weight[tile_view]
    ax = filters[:, :, 0]
    ay = filters[:, :, 1]
    az = filters[:, :, 2]

    starts = jnp.clip(tile_offset - rim, 0, region_rows - win_rows)
    shifts = tile_offset - rim - starts
    windows = jnp.stack(
        [lax.dynamic_slice_in_dim(gathered, starts[j], win_rows, 1) for j in range(tile_count)]
    ).reshape(tile_count, win_x * win_rows, depth)

    kxy = kron_band(ax, ay, block_x, tile_rows, win_rows, win_x * win_rows, 0, shifts[:, None]).reshape(
        tile_count, rank_terms * block_x * tile_rows, win_x * win_rows
    )
    tz = depth_band(az, depth, 128)

    cells = block_x * tile_rows
    part = dot_rounded_data("tmk,tkz->tmz", windows, kxy, False)
    part = part.reshape(tile_count, rank_terms, cells, depth)
    blurred = dot_rounded_data("tqmz,tqzn->tmn", part, tz, True)

    quotient = observed.transpose(1, 0, 2, 3).reshape(tile_count, cells, depth) / blurred

    fxy = kron_band(ax[..., ::-1], ay[..., ::-1], block_x, tile_rows, tile_rows, cells, -rim, -rim).reshape(
        tile_count, rank_terms * cells, cells
    )
    part = dot_rounded_data("tmk,tkz->tmz", quotient, fxy, False)
    part = part.reshape(tile_count, rank_terms, cells, depth)
    correction = jnp.einsum("tqmz,tqnz->tmn", part, tz, precision=MATMUL_PRECISION)
    weighted = (weight[:, None, None] * correction).reshape(tile_count, block_x, tile_rows, depth)

    numerator = jnp.zeros((block_x, region_rows, depth), jnp.float32)
    for j in range(tile_count):
        current = lax.dynamic_slice_in_dim(numerator, tile_offset[j], tile_rows, 1)
        numerator = lax.dynamic_update_slice_in_dim(numerator, current + weighted[j], tile_offset[j], 1)
    own_numerator = lax.psum_scatter(numerator, "tile", scatter_dimension=1, tiled=True)

    me = lax.axis_index("tile")
    rows = me * block_y + jnp.arange(block_y, dtype=jnp.int32)
    inside = (rows[None, :] >= all_offset[:, None]) & (rows[None, :] < all_offset[:, None] + tile_rows)
    own_coverage = jnp.sum(jnp.where(inside, all_weight[:, None], 0.0), axis=0)
    return estimate * (own_numerator + PRIOR_WEIGHT) / (own_coverage[None, :, None] + PRIOR_WEIGHT)


def solution(mesh):
    return jax.shard_map(
        on_device,
        mesh=mesh,
        in_specs=(
            P("region", "tile", None),
            P("region", "tile", None, None),
            P("tile"),
            P("tile"),
            P(),
            P(),
        ),
        out_specs=P("region", "tile", None),
        check_vma=False,
    )
```

```python
import functools

import jax
import jax.numpy as jnp
from jax import lax
from jax.sharding import PartitionSpec as P
from jax.experimental import pallas as pl
from jax.experimental.pallas import tpu as pltpu

PRIOR_WEIGHT = 0.25
MATMUL_PRECISION = lax.Precision.HIGH


def with_halo(cells, sides, width):
    for axis, dim in sides:
        count = lax.axis_size(axis)
        ends = count - 1
        head = lax.slice_in_dim(cells, 0, width, axis=dim)
        tail = lax.slice_in_dim(cells, cells.shape[dim] - width, cells.shape[dim], axis=dim)
        cells = jnp.concatenate(
            [
                lax.ppermute(tail, axis, [(i, (i + 1) % count) for i in range(ends)]),
                cells,
                lax.ppermute(head, axis, [((i + 1) % count, i) for i in range(ends)]),
            ],
            axis=dim,
        )
    return cells


def split_bf16(values):
    high = lax.reduce_precision(values, exponent_bits=8, mantissa_bits=7)
    return high.astype(jnp.bfloat16), (values - high).astype(jnp.bfloat16)


def dot_rounded_data(spec, data, taps, data_first):
    data_high = data.astype(jnp.bfloat16)
    taps_high, taps_low = split_bf16(taps)
    if data_first:
        terms = [(data_high, taps_high), (data_high, taps_low)]
    else:
        terms = [(taps_high, data_high), (taps_low, data_high)]
    return sum(jnp.einsum(spec, a, b, preferred_element_type=jnp.float32) for a, b in terms)


def kron_band(taps_a, taps_b, rows_a, rows_b, span_b, cols, shift_a, shift_b):
    kt = taps_a.shape[-1]
    lead = taps_a.shape[:-1]
    ia = lax.broadcasted_iota(jnp.int32, (rows_a, cols), 0)
    ca = lax.broadcasted_iota(jnp.int32, (rows_a, cols), 1) // span_b
    ib = lax.broadcasted_iota(jnp.int32, (rows_b, cols), 0)
    cb = lax.broadcasted_iota(jnp.int32, (rows_b, cols), 1) % span_b
    da = ca - ia - jnp.asarray(shift_a, jnp.int32)[..., None, None]
    db = cb - ib - jnp.asarray(shift_b, jnp.int32)[..., None, None]
    ea = jnp.zeros(lead + (rows_a, cols), jnp.float32)
    eb = jnp.zeros(lead + (rows_b, cols), jnp.float32)
    for k in range(kt):
        ea = jnp.where(da == k, taps_a[..., k, None, None], ea)
        eb = jnp.where(db == k, taps_b[..., k, None, None], eb)
    return ea[..., :, None, :] * eb[..., None, :, :]


def depth_band(taps, depth, block):
    kt = taps.shape[-1]
    half = (kt - 1) // 2
    i = lax.broadcasted_iota(jnp.int32, (3 * block, block), 0)
    j = lax.broadcasted_iota(jnp.int32, (3 * block, block), 1)
    d = i - block - j + half
    strip = jnp.zeros(taps.shape[:-1] + (3 * block, block), jnp.float32)
    for k in range(kt):
        strip = jnp.where(d == k, taps[..., k, None, None], strip)
    nb = depth // block
    lead = taps.shape[:-1]
    cols = []
    for b in range(nb):
        col = jnp.pad(strip, [(0, 0)] * len(lead) + [(b * block, (nb - 1 - b) * block), (0, 0)])
        cols.append(col[..., block : block + depth, :])
    return jnp.concatenate(cols, axis=-1)


def tile_kernel(win_rows, rank_terms, starts_ref, gathered_ref, kxy_hi, kxy_lo, tz_hi, tz_lo, fxy_hi, fxy_lo,
                fz_hi, fz_lo, obs_ref, out_ref, window, sem):
    j = pl.program_id(0)
    start = pl.multiple_of(starts_ref[j], 8)
    copy = pltpu.make_async_copy(gathered_ref.at[:, pl.ds(start, win_rows), :], window, sem)
    copy.start()
    copy.wait()
    win_x, _, depth = window.shape
    data = window[...].reshape(win_x * win_rows, depth).astype(jnp.bfloat16)
    f32 = jnp.float32
    part = jnp.dot(kxy_hi[0], data, preferred_element_type=f32) + jnp.dot(kxy_lo[0], data, preferred_element_type=f32)
    cells = part.shape[0] // rank_terms
    blurred = None
    for q in range(rank_terms):
        p = part[q * cells : (q + 1) * cells].astype(jnp.bfloat16)
        term = jnp.dot(p, tz_hi[0, q], preferred_element_type=f32) + jnp.dot(p, tz_lo[0, q], preferred_element_type=f32)
        blurred = term if blurred is None else blurred + term
    quotient = (obs_ref[0] / blurred).astype(jnp.bfloat16)
    part = jnp.dot(fxy_hi[0], quotient, preferred_element_type=f32) + jnp.dot(fxy_lo[0], quotient, preferred_element_type=f32)
    correction = None
    for q in range(rank_terms):
        c = part[q * cells : (q + 1) * cells]
        c_hi = c.astype(jnp.bfloat16)
        c_lo = (c - c_hi.astype(f32)).astype(jnp.bfloat16)
        term = (
            jnp.dot(c_hi, fz_hi[0, q], preferred_element_type=f32)
            + jnp.dot(c_lo, fz_hi[0, q], preferred_element_type=f32)
            + jnp.dot(c_hi, fz_lo[0, q], preferred_element_type=f32)
        )
        correction = term if correction is None else correction + term
    out_ref[0] = correction


def on_device(estimate, observed, tile_offset, tile_view, psf_taps, view_weight):
    kt = psf_taps.shape[3]
    rim = (kt - 1) // 2
    block_x, block_y, depth = estimate.shape
    tile_count = observed.shape[1]
    tile_rows = observed.shape[2]
    rank_terms = psf_taps.shape[1]
    group_size = lax.axis_size("tile")
    region_rows = block_y * group_size
    win_rows = -(-(tile_rows + 2 * rim + 7) // 8) * 8
    win_x = block_x + 2 * rim

    tile_info = jnp.stack([tile_offset.astype(jnp.float32), view_weight[tile_view]], axis=1)
    all_info = lax.all_gather(tile_info, "tile", tiled=True)
    all_offset = all_info[:, 0].astype(jnp.int32)
    all_weight = all_info[:, 1]

    rimmed = with_halo(estimate, (("region", 0),), rim)
    gathered = lax.all_gather(rimmed, "tile", axis=1, tiled=True)

    filters = psf_taps[tile_view]
    weight = view_weight[tile_view]
    ax = filters[:, :, 0]
    ay = filters[:, :, 1]
    az = filters[:, :, 2]

    starts = jnp.clip(((tile_offset - rim) // 8) * 8, 0, region_rows - win_rows)
    shifts = tile_offset - rim - starts
    kxy = kron_band(ax, ay, block_x, tile_rows, win_rows, win_x * win_rows, 0, shifts[:, None]).reshape(
        tile_count, rank_terms * block_x * tile_rows, win_x * win_rows
    )
    tz = depth_band(az, depth, 128)

    cells = block_x * tile_rows
    fxy = kron_band(ax[..., ::-1], ay[..., ::-1], block_x, tile_rows, tile_rows, cells, -rim, -rim).reshape(
        tile_count, rank_terms * cells, cells
    )
    obs = observed.transpose(1, 0, 2, 3).reshape(tile_count, cells, depth)
    kxy_hi, kxy_lo = split_bf16(kxy)
    tz_hi, tz_lo = split_bf16(tz)
    fz_hi, fz_lo = split_bf16(jnp.swapaxes(tz, -1, -2))
    fxy_hi, fxy_lo = split_bf16(fxy)
    per_tile = lambda *shape: pl.BlockSpec((1,) + shape, lambda j, s: (j,) + (0,) * len(shape))
    correction = pl.pallas_call(
        functools.partial(tile_kernel, win_rows, rank_terms),
        grid_spec=pltpu.PrefetchScalarGridSpec(
            num_scalar_prefetch=1,
            grid=(tile_count,),
            in_specs=[
                pl.BlockSpec(memory_space=pl.ANY),
                per_tile(rank_terms * cells, win_x * win_rows),
                per_tile(rank_terms * cells, win_x * win_rows),
                per_tile(rank_terms, depth, depth),
                per_tile(rank_terms, depth, depth),
                per_tile(rank_terms * cells, cells),
                per_tile(rank_terms * cells, cells),
                per_tile(rank_terms, depth, depth),
                per_tile(rank_terms, depth, depth),
                per_tile(cells, depth),
            ],
            out_specs=per_tile(cells, depth),
            scratch_shapes=[pltpu.VMEM((win_x, win_rows, depth), jnp.float32), pltpu.SemaphoreType.DMA(())],
        ),
        out_shape=jax.ShapeDtypeStruct((tile_count, cells, depth), jnp.float32),
        compiler_params=pltpu.CompilerParams(vmem_limit_bytes=60 * 1024 * 1024),
    )(starts, gathered, kxy_hi, kxy_lo, tz_hi, tz_lo, fxy_hi, fxy_lo, fz_hi, fz_lo, obs)
    weighted = (weight[:, None, None] * correction).reshape(tile_count, block_x, tile_rows, depth)

    numerator = jnp.zeros((block_x, region_rows, depth), jnp.float32)
    for j in range(tile_count):
        current = lax.dynamic_slice_in_dim(numerator, tile_offset[j], tile_rows, 1)
        numerator = lax.dynamic_update_slice_in_dim(numerator, current + weighted[j], tile_offset[j], 1)
    own_numerator = lax.psum_scatter(numerator, "tile", scatter_dimension=1, tiled=True)

    me = lax.axis_index("tile")
    rows = me * block_y + jnp.arange(block_y, dtype=jnp.int32)
    inside = (rows[None, :] >= all_offset[:, None]) & (rows[None, :] < all_offset[:, None] + tile_rows)
    own_coverage = jnp.sum(jnp.where(inside, all_weight[:, None], 0.0), axis=0)
    return estimate * (own_numerator + PRIOR_WEIGHT) / (own_coverage[None, :, None] + PRIOR_WEIGHT)


def solution(mesh):
    return jax.shard_map(
        on_device,
        mesh=mesh,
        in_specs=(
            P("region", "tile", None),
            P("region", "tile", None, None),
            P("tile"),
            P("tile"),
            P(),
            P(),
        ),
        out_specs=P("region", "tile", None),
        check_vma=False,
    )
```

```python
import functools

import jax
import jax.numpy as jnp
from jax import lax
from jax.sharding import PartitionSpec as P
from jax.experimental import pallas as pl
from jax.experimental.pallas import tpu as pltpu

PRIOR_WEIGHT = 0.25
MATMUL_PRECISION = lax.Precision.HIGH


def with_halo(cells, sides, width):
    for axis, dim in sides:
        count = lax.axis_size(axis)
        ends = count - 1
        head = lax.slice_in_dim(cells, 0, width, axis=dim)
        tail = lax.slice_in_dim(cells, cells.shape[dim] - width, cells.shape[dim], axis=dim)
        cells = jnp.concatenate(
            [
                lax.ppermute(tail, axis, [(i, (i + 1) % count) for i in range(ends)]),
                cells,
                lax.ppermute(head, axis, [((i + 1) % count, i) for i in range(ends)]),
            ],
            axis=dim,
        )
    return cells


def split_bf16(values):
    high = lax.reduce_precision(values, exponent_bits=8, mantissa_bits=7)
    return high.astype(jnp.bfloat16), (values - high).astype(jnp.bfloat16)


def dot_rounded_data(spec, data, taps, data_first):
    data_high = data.astype(jnp.bfloat16)
    taps_high, taps_low = split_bf16(taps)
    if data_first:
        terms = [(data_high, taps_high), (data_high, taps_low)]
    else:
        terms = [(taps_high, data_high), (taps_low, data_high)]
    return sum(jnp.einsum(spec, a, b, preferred_element_type=jnp.float32) for a, b in terms)


def kron_band(taps_a, taps_b, rows_a, rows_b, span_b, cols, shift_a, shift_b):
    kt = taps_a.shape[-1]
    lead = taps_a.shape[:-1]
    ia = lax.broadcasted_iota(jnp.int32, (rows_a, cols), 0)
    ca = lax.broadcasted_iota(jnp.int32, (rows_a, cols), 1) // span_b
    ib = lax.broadcasted_iota(jnp.int32, (rows_b, cols), 0)
    cb = lax.broadcasted_iota(jnp.int32, (rows_b, cols), 1) % span_b
    da = ca - ia - jnp.asarray(shift_a, jnp.int32)[..., None, None]
    db = cb - ib - jnp.asarray(shift_b, jnp.int32)[..., None, None]
    ea = jnp.zeros(lead + (rows_a, cols), jnp.float32)
    eb = jnp.zeros(lead + (rows_b, cols), jnp.float32)
    for k in range(kt):
        ea = jnp.where(da == k, taps_a[..., k, None, None], ea)
        eb = jnp.where(db == k, taps_b[..., k, None, None], eb)
    return ea[..., :, None, :] * eb[..., None, :, :]


def depth_band(taps, depth, block):
    kt = taps.shape[-1]
    half = (kt - 1) // 2
    i = lax.broadcasted_iota(jnp.int32, (3 * block, block), 0)
    j = lax.broadcasted_iota(jnp.int32, (3 * block, block), 1)
    d = i - block - j + half
    strip = jnp.zeros(taps.shape[:-1] + (3 * block, block), jnp.float32)
    for k in range(kt):
        strip = jnp.where(d == k, taps[..., k, None, None], strip)
    nb = depth // block
    lead = taps.shape[:-1]
    cols = []
    for b in range(nb):
        col = jnp.pad(strip, [(0, 0)] * len(lead) + [(b * block, (nb - 1 - b) * block), (0, 0)])
        cols.append(col[..., block : block + depth, :])
    return jnp.concatenate(cols, axis=-1)


def tile_kernel(win_rows, rank_terms, starts_ref, gathered_ref, kxy_hi, kxy_lo, tz_hi, tz_lo, fxy_hi, fxy_lo,
                obs_ref, out_ref, window, sem):
    j = pl.program_id(0)
    start = pl.multiple_of(starts_ref[j], 8)
    copy = pltpu.make_async_copy(gathered_ref.at[:, pl.ds(start, win_rows), :], window, sem)
    copy.start()
    copy.wait()
    win_x, _, depth = window.shape
    data = window[...].reshape(win_x * win_rows, depth).astype(jnp.bfloat16)
    f32 = jnp.float32
    part = jnp.dot(kxy_hi[0], data, preferred_element_type=f32) + jnp.dot(kxy_lo[0], data, preferred_element_type=f32)
    cells = part.shape[0] // rank_terms
    blurred = None
    for q in range(rank_terms):
        p = part[q * cells : (q + 1) * cells].astype(jnp.bfloat16)
        term = jnp.dot(p, tz_hi[0, q], preferred_element_type=f32) + jnp.dot(p, tz_lo[0, q], preferred_element_type=f32)
        blurred = term if blurred is None else blurred + term
    quotient = (obs_ref[0] / blurred).astype(jnp.bfloat16)
    part = jnp.dot(fxy_hi[0], quotient, preferred_element_type=f32) + jnp.dot(fxy_lo[0], quotient, preferred_element_type=f32)
    correction = None
    for q in range(rank_terms):
        c = part[q * cells : (q + 1) * cells]
        c_hi = c.astype(jnp.bfloat16)
        c_lo = (c - c_hi.astype(f32)).astype(jnp.bfloat16)
        nt = (((1,), (1,)), ((), ()))
        term = (
            lax.dot_general(c_hi, tz_hi[0, q], nt, preferred_element_type=f32)
            + lax.dot_general(c_lo, tz_hi[0, q], nt, preferred_element_type=f32)
            + lax.dot_general(c_hi, tz_lo[0, q], nt, preferred_element_type=f32)
        )
        correction = term if correction is None else correction + term
    out_ref[0] = correction


def on_device(estimate, observed, tile_offset, tile_view, psf_taps, view_weight):
    kt = psf_taps.shape[3]
    rim = (kt - 1) // 2
    block_x, block_y, depth = estimate.shape
    tile_count = observed.shape[1]
    tile_rows = observed.shape[2]
    rank_terms = psf_taps.shape[1]
    group_size = lax.axis_size("tile")
    region_rows = block_y * group_size
    win_rows = -(-(tile_rows + 2 * rim + 7) // 8) * 8
    win_x = block_x + 2 * rim

    tile_info = jnp.stack([tile_offset.astype(jnp.float32), view_weight[tile_view]], axis=1)
    all_info = lax.all_gather(tile_info, "tile", tiled=True)
    all_offset = all_info[:, 0].astype(jnp.int32)
    all_weight = all_info[:, 1]

    rimmed = with_halo(estimate, (("region", 0),), rim)
    gathered = lax.all_gather(rimmed, "tile", axis=1, tiled=True)

    filters = psf_taps[tile_view]
    weight = view_weight[tile_view]
    ax = filters[:, :, 0]
    ay = filters[:, :, 1]
    az = filters[:, :, 2]

    starts = jnp.clip(((tile_offset - rim) // 8) * 8, 0, region_rows - win_rows)
    shifts = tile_offset - rim - starts
    kxy = kron_band(ax, ay, block_x, tile_rows, win_rows, win_x * win_rows, 0, shifts[:, None]).reshape(
        tile_count, rank_terms * block_x * tile_rows, win_x * win_rows
    )
    tz = depth_band(az, depth, 128)

    cells = block_x * tile_rows
    fxy = kron_band(ax[..., ::-1], ay[..., ::-1], block_x, tile_rows, tile_rows, cells, -rim, -rim).reshape(
        tile_count, rank_terms * cells, cells
    )
    obs = observed.transpose(1, 0, 2, 3).reshape(tile_count, cells, depth)
    kxy_hi, kxy_lo = split_bf16(kxy)
    tz_hi, tz_lo = split_bf16(tz)
    fxy_hi, fxy_lo = split_bf16(fxy)
    per_tile = lambda *shape: pl.BlockSpec((1,) + shape, lambda j, s: (j,) + (0,) * len(shape))
    correction = pl.pallas_call(
        functools.partial(tile_kernel, win_rows, rank_terms),
        grid_spec=pltpu.PrefetchScalarGridSpec(
            num_scalar_prefetch=1,
            grid=(tile_count,),
            in_specs=[
                pl.BlockSpec(memory_space=pl.ANY),
                per_tile(rank_terms * cells, win_x * win_rows),
                per_tile(rank_terms * cells, win_x * win_rows),
                per_tile(rank_terms, depth, depth),
                per_tile(rank_terms, depth, depth),
                per_tile(rank_terms * cells, cells),
                per_tile(rank_terms * cells, cells),
                per_tile(cells, depth),
            ],
            out_specs=per_tile(cells, depth),
            scratch_shapes=[pltpu.VMEM((win_x, win_rows, depth), jnp.float32), pltpu.SemaphoreType.DMA(())],
        ),
        out_shape=jax.ShapeDtypeStruct((tile_count, cells, depth), jnp.float32),
        compiler_params=pltpu.CompilerParams(vmem_limit_bytes=60 * 1024 * 1024),
    )(starts, gathered, kxy_hi, kxy_lo, tz_hi, tz_lo, fxy_hi, fxy_lo, obs)
    weighted = (weight[:, None, None] * correction).reshape(tile_count, block_x, tile_rows, depth)

    numerator = jnp.zeros((block_x, region_rows, depth), jnp.float32)
    for j in range(tile_count):
        current = lax.dynamic_slice_in_dim(numerator, tile_offset[j], tile_rows, 1)
        numerator = lax.dynamic_update_slice_in_dim(numerator, current + weighted[j], tile_offset[j], 1)
    own_numerator = lax.psum_scatter(numerator, "tile", scatter_dimension=1, tiled=True)

    me = lax.axis_index("tile")
    rows = me * block_y + jnp.arange(block_y, dtype=jnp.int32)
    inside = (rows[None, :] >= all_offset[:, None]) & (rows[None, :] < all_offset[:, None] + tile_rows)
    own_coverage = jnp.sum(jnp.where(inside, all_weight[:, None], 0.0), axis=0)
    return estimate * (own_numerator + PRIOR_WEIGHT) / (own_coverage[None, :, None] + PRIOR_WEIGHT)


def solution(mesh):
    return jax.shard_map(
        on_device,
        mesh=mesh,
        in_specs=(
            P("region", "tile", None),
            P("region", "tile", None, None),
            P("tile"),
            P("tile"),
            P(),
            P(),
        ),
        out_specs=P("region", "tile", None),
        check_vma=False,
    )
```

```python
import functools

import jax
import jax.numpy as jnp
from jax import lax
from jax.sharding import PartitionSpec as P
from jax.experimental import pallas as pl
from jax.experimental.pallas import tpu as pltpu

PRIOR_WEIGHT = 0.25
MATMUL_PRECISION = lax.Precision.HIGH


def with_halo(cells, sides, width):
    for axis, dim in sides:
        count = lax.axis_size(axis)
        ends = count - 1
        head = lax.slice_in_dim(cells, 0, width, axis=dim)
        tail = lax.slice_in_dim(cells, cells.shape[dim] - width, cells.shape[dim], axis=dim)
        cells = jnp.concatenate(
            [
                lax.ppermute(tail, axis, [(i, (i + 1) % count) for i in range(ends)]),
                cells,
                lax.ppermute(head, axis, [((i + 1) % count, i) for i in range(ends)]),
            ],
            axis=dim,
        )
    return cells


def split_bf16(values):
    high = lax.reduce_precision(values, exponent_bits=8, mantissa_bits=7)
    return high.astype(jnp.bfloat16), (values - high).astype(jnp.bfloat16)


def dot_rounded_data(spec, data, taps, data_first):
    data_high = data.astype(jnp.bfloat16)
    taps_high, taps_low = split_bf16(taps)
    if data_first:
        terms = [(data_high, taps_high), (data_high, taps_low)]
    else:
        terms = [(taps_high, data_high), (taps_low, data_high)]
    return sum(jnp.einsum(spec, a, b, preferred_element_type=jnp.float32) for a, b in terms)


def kron_band(taps_a, taps_b, rows_a, rows_b, span_b, cols, shift_a, shift_b):
    kt = taps_a.shape[-1]
    lead = taps_a.shape[:-1]
    ia = lax.broadcasted_iota(jnp.int32, (rows_a, cols), 0)
    ca = lax.broadcasted_iota(jnp.int32, (rows_a, cols), 1) // span_b
    ib = lax.broadcasted_iota(jnp.int32, (rows_b, cols), 0)
    cb = lax.broadcasted_iota(jnp.int32, (rows_b, cols), 1) % span_b
    da = ca - ia - jnp.asarray(shift_a, jnp.int32)[..., None, None]
    db = cb - ib - jnp.asarray(shift_b, jnp.int32)[..., None, None]
    ea = jnp.zeros(lead + (rows_a, cols), jnp.float32)
    eb = jnp.zeros(lead + (rows_b, cols), jnp.float32)
    for k in range(kt):
        ea = jnp.where(da == k, taps_a[..., k, None, None], ea)
        eb = jnp.where(db == k, taps_b[..., k, None, None], eb)
    return ea[..., :, None, :] * eb[..., None, :, :]


def depth_band(taps, depth, block):
    kt = taps.shape[-1]
    half = (kt - 1) // 2
    i = lax.broadcasted_iota(jnp.int32, (3 * block, block), 0)
    j = lax.broadcasted_iota(jnp.int32, (3 * block, block), 1)
    d = i - block - j + half
    strip = jnp.zeros(taps.shape[:-1] + (3 * block, block), jnp.float32)
    for k in range(kt):
        strip = jnp.where(d == k, taps[..., k, None, None], strip)
    nb = depth // block
    lead = taps.shape[:-1]
    cols = []
    for b in range(nb):
        col = jnp.pad(strip, [(0, 0)] * len(lead) + [(b * block, (nb - 1 - b) * block), (0, 0)])
        cols.append(col[..., block : block + depth, :])
    return jnp.concatenate(cols, axis=-1)


def tile_kernel(win_rows, rank_terms, starts_ref, gathered_ref, kxy_hi, kxy_lo, tz_hi, tz_lo, fxy_hi, fxy_lo,
                fz_hi, fz_lo, obs_ref, out_ref, window, sem):
    j = pl.program_id(0)
    start = pl.multiple_of(starts_ref[j], 8)
    copy = pltpu.make_async_copy(gathered_ref.at[:, pl.ds(start, win_rows), :], window, sem)
    copy.start()
    copy.wait()
    win_x, _, depth = window.shape
    data = window[...].reshape(win_x * win_rows, depth).astype(jnp.bfloat16)
    f32 = jnp.float32
    part = jnp.dot(kxy_hi[0], data, preferred_element_type=f32) + jnp.dot(kxy_lo[0], data, preferred_element_type=f32)
    cells = part.shape[0] // rank_terms
    depth_blocks = depth // 128

    def along_depth(rows, strip_hi, strip_lo, q, passes):
        out = []
        for b in range(depth_blocks):
            lo = max(b - 1, 0)
            hi = min(b + 2, depth_blocks)
            sub = slice((lo - b + 1) * 128, (hi - b + 1) * 128)
            cols = slice(lo * 128, hi * 128)
            acc = None
            for a, m in passes(rows[:, cols], strip_hi[0, q, sub], strip_lo[0, q, sub]):
                t = jnp.dot(a, m, preferred_element_type=f32)
                acc = t if acc is None else acc + t
            out.append(acc)
        return jnp.concatenate(out, axis=1)

    two = lambda a, mh, ml: [(a, mh), (a, ml)]
    blurred = None
    for q in range(rank_terms):
        p = part[q * cells : (q + 1) * cells].astype(jnp.bfloat16)
        term = along_depth(p, tz_hi, tz_lo, q, two)
        blurred = term if blurred is None else blurred + term
    quotient = (obs_ref[0] / blurred).astype(jnp.bfloat16)
    part = jnp.dot(fxy_hi[0], quotient, preferred_element_type=f32) + jnp.dot(fxy_lo[0], quotient, preferred_element_type=f32)
    def three(a, mh, ml):
        a_hi = a.astype(jnp.bfloat16)
        a_lo = (a - a_hi.astype(f32)).astype(jnp.bfloat16)
        return [(a_hi, mh), (a_lo, mh), (a_hi, ml)]

    correction = None
    for q in range(rank_terms):
        c = part[q * cells : (q + 1) * cells]
        term = along_depth(c, fz_hi, fz_lo, q, three)
        correction = term if correction is None else correction + term
    out_ref[0] = correction


def on_device(estimate, observed, tile_offset, tile_view, psf_taps, view_weight):
    kt = psf_taps.shape[3]
    rim = (kt - 1) // 2
    block_x, block_y, depth = estimate.shape
    tile_count = observed.shape[1]
    tile_rows = observed.shape[2]
    rank_terms = psf_taps.shape[1]
    group_size = lax.axis_size("tile")
    region_rows = block_y * group_size
    win_rows = -(-(tile_rows + 2 * rim + 7) // 8) * 8
    win_x = block_x + 2 * rim

    tile_info = jnp.stack([tile_offset.astype(jnp.float32), view_weight[tile_view]], axis=1)
    all_info = lax.all_gather(tile_info, "tile", tiled=True)
    all_offset = all_info[:, 0].astype(jnp.int32)
    all_weight = all_info[:, 1]

    rimmed = with_halo(estimate, (("region", 0),), rim)
    gathered = lax.all_gather(rimmed, "tile", axis=1, tiled=True)

    filters = psf_taps[tile_view]
    weight = view_weight[tile_view]
    ax = filters[:, :, 0]
    ay = filters[:, :, 1]
    az = filters[:, :, 2]

    starts = jnp.clip(((tile_offset - rim) // 8) * 8, 0, region_rows - win_rows)
    shifts = tile_offset - rim - starts
    kxy = kron_band(ax, ay, block_x, tile_rows, win_rows, win_x * win_rows, 0, shifts[:, None]).reshape(
        tile_count, rank_terms * block_x * tile_rows, win_x * win_rows
    )
    si = lax.broadcasted_iota(jnp.int32, (3 * 128, 128), 0)
    sj = lax.broadcasted_iota(jnp.int32, (3 * 128, 128), 1)
    sd = si - 128 - sj + rim
    strip = jnp.zeros((tile_count, rank_terms, 3 * 128, 128), jnp.float32)
    for k in range(kt):
        strip = jnp.where(sd == k, az[..., k, None, None], strip)

    cells = block_x * tile_rows
    fxy = kron_band(ax[..., ::-1], ay[..., ::-1], block_x, tile_rows, tile_rows, cells, -rim, -rim).reshape(
        tile_count, rank_terms * cells, cells
    )
    fxy = weight[:, None, None] * fxy
    obs = observed.transpose(1, 0, 2, 3).reshape(tile_count, cells, depth)
    kxy_hi, kxy_lo = split_bf16(kxy)
    tz_hi, tz_lo = split_bf16(strip)
    fz_hi, fz_lo = split_bf16(strip[..., ::-1, ::-1])
    fxy_hi, fxy_lo = split_bf16(fxy)
    per_tile = lambda *shape: pl.BlockSpec((1,) + shape, lambda j, s: (j,) + (0,) * len(shape))
    correction = pl.pallas_call(
        functools.partial(tile_kernel, win_rows, rank_terms),
        grid_spec=pltpu.PrefetchScalarGridSpec(
            num_scalar_prefetch=1,
            grid=(tile_count,),
            in_specs=[
                pl.BlockSpec(memory_space=pl.ANY),
                per_tile(rank_terms * cells, win_x * win_rows),
                per_tile(rank_terms * cells, win_x * win_rows),
                per_tile(rank_terms, 3 * 128, 128),
                per_tile(rank_terms, 3 * 128, 128),
                per_tile(rank_terms * cells, cells),
                per_tile(rank_terms * cells, cells),
                per_tile(rank_terms, 3 * 128, 128),
                per_tile(rank_terms, 3 * 128, 128),
                per_tile(cells, depth),
            ],
            out_specs=per_tile(cells, depth),
            scratch_shapes=[pltpu.VMEM((win_x, win_rows, depth), jnp.float32), pltpu.SemaphoreType.DMA(())],
        ),
        out_shape=jax.ShapeDtypeStruct((tile_count, cells, depth), jnp.float32),
        compiler_params=pltpu.CompilerParams(vmem_limit_bytes=60 * 1024 * 1024),
    )(starts, gathered, kxy_hi, kxy_lo, tz_hi, tz_lo, fxy_hi, fxy_lo, fz_hi, fz_lo, obs)
    weighted = correction.reshape(tile_count, block_x, tile_rows, depth)

    numerator = jnp.zeros((block_x, region_rows, depth), jnp.float32)
    for j in range(tile_count):
        current = lax.dynamic_slice_in_dim(numerator, tile_offset[j], tile_rows, 1)
        numerator = lax.dynamic_update_slice_in_dim(numerator, current + weighted[j], tile_offset[j], 1)
    own_numerator = lax.psum_scatter(numerator, "tile", scatter_dimension=1, tiled=True)

    me = lax.axis_index("tile")
    rows = me * block_y + jnp.arange(block_y, dtype=jnp.int32)
    inside = (rows[None, :] >= all_offset[:, None]) & (rows[None, :] < all_offset[:, None] + tile_rows)
    own_coverage = jnp.sum(jnp.where(inside, all_weight[:, None], 0.0), axis=0)
    return estimate * (own_numerator + PRIOR_WEIGHT) / (own_coverage[None, :, None] + PRIOR_WEIGHT)


def solution(mesh):
    return jax.shard_map(
        on_device,
        mesh=mesh,
        in_specs=(
            P("region", "tile", None),
            P("region", "tile", None, None),
            P("tile"),
            P("tile"),
            P(),
            P(),
        ),
        out_specs=P("region", "tile", None),
        check_vma=False,
    )
```

```python
import jax
import jax.numpy as jnp
from jax import lax
from jax.sharding import PartitionSpec as P

PRIOR_WEIGHT = 0.25
MATMUL_PRECISION = lax.Precision.HIGH


def with_halo(cells, sides, width):
    for axis, dim in sides:
        count = lax.axis_size(axis)
        ends = count - 1
        head = lax.slice_in_dim(cells, 0, width, axis=dim)
        tail = lax.slice_in_dim(cells, cells.shape[dim] - width, cells.shape[dim], axis=dim)
        cells = jnp.concatenate(
            [
                lax.ppermute(tail, axis, [(i, (i + 1) % count) for i in range(ends)]),
                cells,
                lax.ppermute(head, axis, [((i + 1) % count, i) for i in range(ends)]),
            ],
            axis=dim,
        )
    return cells


def split_bf16(values):
    high = lax.reduce_precision(values, exponent_bits=8, mantissa_bits=7)
    return high.astype(jnp.bfloat16), (values - high).astype(jnp.bfloat16)


def dot_rounded_data(spec, data, taps, data_first):
    data_high = data.astype(jnp.bfloat16)
    taps_high, taps_low = split_bf16(taps)
    if data_first:
        terms = [(data_high, taps_high), (data_high, taps_low)]
    else:
        terms = [(taps_high, data_high), (taps_low, data_high)]
    return sum(jnp.einsum(spec, a, b, preferred_element_type=jnp.float32) for a, b in terms)


def kron_band(taps_a, taps_b, rows_a, rows_b, span_b, cols, shift_a, shift_b):
    kt = taps_a.shape[-1]
    lead = taps_a.shape[:-1]
    ia = lax.broadcasted_iota(jnp.int32, (rows_a, cols), 0)
    ca = lax.broadcasted_iota(jnp.int32, (rows_a, cols), 1) // span_b
    ib = lax.broadcasted_iota(jnp.int32, (rows_b, cols), 0)
    cb = lax.broadcasted_iota(jnp.int32, (rows_b, cols), 1) % span_b
    da = ca - ia - jnp.asarray(shift_a, jnp.int32)[..., None, None]
    db = cb - ib - jnp.asarray(shift_b, jnp.int32)[..., None, None]
    ea = jnp.zeros(lead + (rows_a, cols), jnp.float32)
    eb = jnp.zeros(lead + (rows_b, cols), jnp.float32)
    for k in range(kt):
        ea = jnp.where(da == k, taps_a[..., k, None, None], ea)
        eb = jnp.where(db == k, taps_b[..., k, None, None], eb)
    return ea[..., :, None, :] * eb[..., None, :, :]


def depth_band(taps, depth, block):
    kt = taps.shape[-1]
    half = (kt - 1) // 2
    i = lax.broadcasted_iota(jnp.int32, (3 * block, block), 0)
    j = lax.broadcasted_iota(jnp.int32, (3 * block, block), 1)
    d = i - block - j + half
    strip = jnp.zeros(taps.shape[:-1] + (3 * block, block), jnp.float32)
    for k in range(kt):
        strip = jnp.where(d == k, taps[..., k, None, None], strip)
    nb = depth // block
    lead = taps.shape[:-1]
    cols = []
    for b in range(nb):
        col = jnp.pad(strip, [(0, 0)] * len(lead) + [(b * block, (nb - 1 - b) * block), (0, 0)])
        cols.append(col[..., block : block + depth, :])
    return jnp.concatenate(cols, axis=-1)


def on_device(estimate, observed, tile_offset, tile_view, psf_taps, view_weight):
    kt = psf_taps.shape[3]
    rim = (kt - 1) // 2
    block_x, block_y, depth = estimate.shape
    tile_count = observed.shape[1]
    tile_rows = observed.shape[2]
    rank_terms = psf_taps.shape[1]
    group_size = lax.axis_size("tile")
    region_rows = block_y * group_size
    win_rows = -(-(tile_rows + 2 * rim) // 8) * 8
    win_x = block_x + 2 * rim

    tile_info = jnp.stack([tile_offset.astype(jnp.float32), view_weight[tile_view]], axis=1)
    all_info = lax.all_gather(tile_info, "tile", tiled=True)
    all_offset = all_info[:, 0].astype(jnp.int32)
    all_weight = all_info[:, 1]

    rimmed = with_halo(estimate, (("region", 0),), rim)
    gathered = lax.all_gather(rimmed, "tile", axis=1, tiled=True)

    filters = psf_taps[tile_view]
    weight = view_weight[tile_view]
    ax = filters[:, :, 0]
    ay = filters[:, :, 1]
    az = filters[:, :, 2]

    starts = jnp.clip(tile_offset - rim, 0, region_rows - win_rows)
    shifts = tile_offset - rim - starts
    windows = jnp.stack(
        [lax.dynamic_slice_in_dim(gathered, starts[j], win_rows, 1) for j in range(tile_count)]
    ).reshape(tile_count, win_x * win_rows, depth)

    kxy = kron_band(ax, ay, block_x, tile_rows, win_rows, win_x * win_rows, 0, shifts[:, None]).reshape(
        tile_count, rank_terms * block_x * tile_rows, win_x * win_rows
    )
    tz = depth_band(az, depth, 128)

    cells = block_x * tile_rows
    part = jnp.einsum("tmk,tkz->tmz", kxy, windows, precision=MATMUL_PRECISION)
    part = part.reshape(tile_count, rank_terms, cells, depth)
    blurred = dot_rounded_data("tqmz,tqzn->tmn", part, tz, True)

    quotient = observed.transpose(1, 0, 2, 3).reshape(tile_count, cells, depth) / blurred

    ry = ay[..., ::-1]
    rx = ax[..., ::-1]
    ci = lax.broadcasted_iota(jnp.int32, (tile_rows, cells), 1)
    fy_d = ci % tile_rows - lax.broadcasted_iota(jnp.int32, (tile_rows, cells), 0) + rim
    fx_d = lax.broadcasted_iota(jnp.int32, (block_x, cells), 1) // tile_rows - lax.broadcasted_iota(
        jnp.int32, (block_x, cells), 0
    ) + rim
    fy_e = jnp.zeros((tile_count, rank_terms, tile_rows, cells), jnp.float32)
    fx_e = jnp.zeros((tile_count, rank_terms, block_x, cells), jnp.float32)
    for k in range(kt):
        fy_e = jnp.where(fy_d == k, ry[..., k, None, None], fy_e)
        fx_e = jnp.where(fx_d == k, rx[..., k, None, None], fx_e)
    fxy = (fy_e[:, :, :, None, :] * fx_e[:, :, None, :, :]).reshape(tile_count, rank_terms * cells, cells)
    part = dot_rounded_data("tmk,tkz->tmz", quotient, fxy, False)
    part = part.reshape(tile_count, rank_terms, cells, depth)
    correction = jnp.einsum("tqmz,tqnz->tmn", part, tz, precision=MATMUL_PRECISION)
    weighted = (weight[:, None, None] * correction).reshape(tile_count, tile_rows, block_x, depth)
    rows_all = lax.broadcasted_iota(jnp.int32, (tile_count, region_rows, tile_rows), 1)
    rows_tile = lax.broadcasted_iota(jnp.int32, (tile_count, region_rows, tile_rows), 2)
    place = (rows_all - rows_tile == tile_offset[:, None, None]).astype(jnp.float32)
    numerator = jnp.einsum("jYy,jyxz->Yxz", place, weighted, precision=lax.Precision.HIGHEST)
    own_numerator = lax.psum_scatter(numerator, "tile", scatter_dimension=0, tiled=True).transpose(1, 0, 2)

    me = lax.axis_index("tile")
    rows = me * block_y + jnp.arange(block_y, dtype=jnp.int32)
    inside = (rows[None, :] >= all_offset[:, None]) & (rows[None, :] < all_offset[:, None] + tile_rows)
    own_coverage = jnp.sum(jnp.where(inside, all_weight[:, None], 0.0), axis=0)
    return estimate * (own_numerator + PRIOR_WEIGHT) / (own_coverage[None, :, None] + PRIOR_WEIGHT)


def solution(mesh):
    return jax.shard_map(
        on_device,
        mesh=mesh,
        in_specs=(
            P("region", "tile", None),
            P("region", "tile", None, None),
            P("tile"),
            P("tile"),
            P(),
            P(),
        ),
        out_specs=P("region", "tile", None),
        check_vma=False,
    )
```

```python
import jax
import jax.numpy as jnp
from jax import lax
from jax.sharding import PartitionSpec as P

PRIOR_WEIGHT = 0.25
MATMUL_PRECISION = lax.Precision.HIGH


def with_halo(cells, sides, width):
    for axis, dim in sides:
        count = lax.axis_size(axis)
        ends = count - 1
        head = lax.slice_in_dim(cells, 0, width, axis=dim)
        tail = lax.slice_in_dim(cells, cells.shape[dim] - width, cells.shape[dim], axis=dim)
        cells = jnp.concatenate(
            [
                lax.ppermute(tail, axis, [(i, (i + 1) % count) for i in range(ends)]),
                cells,
                lax.ppermute(head, axis, [((i + 1) % count, i) for i in range(ends)]),
            ],
            axis=dim,
        )
    return cells


def split_bf16(values):
    high = lax.reduce_precision(values, exponent_bits=8, mantissa_bits=7)
    return high.astype(jnp.bfloat16), (values - high).astype(jnp.bfloat16)


def dot_rounded_data(spec, data, taps, data_first):
    data_high = data.astype(jnp.bfloat16)
    taps_high, taps_low = split_bf16(taps)
    if data_first:
        terms = [(data_high, taps_high), (data_high, taps_low)]
    else:
        terms = [(taps_high, data_high), (taps_low, data_high)]
    return sum(jnp.einsum(spec, a, b, preferred_element_type=jnp.float32) for a, b in terms)


def kron_band(taps_a, taps_b, rows_a, rows_b, span_b, cols, shift_a, shift_b):
    kt = taps_a.shape[-1]
    lead = taps_a.shape[:-1]
    ia = lax.broadcasted_iota(jnp.int32, (rows_a, cols), 0)
    ca = lax.broadcasted_iota(jnp.int32, (rows_a, cols), 1) // span_b
    ib = lax.broadcasted_iota(jnp.int32, (rows_b, cols), 0)
    cb = lax.broadcasted_iota(jnp.int32, (rows_b, cols), 1) % span_b
    da = ca - ia - jnp.asarray(shift_a, jnp.int32)[..., None, None]
    db = cb - ib - jnp.asarray(shift_b, jnp.int32)[..., None, None]
    ea = jnp.zeros(lead + (rows_a, cols), jnp.float32)
    eb = jnp.zeros(lead + (rows_b, cols), jnp.float32)
    for k in range(kt):
        ea = jnp.where(da == k, taps_a[..., k, None, None], ea)
        eb = jnp.where(db == k, taps_b[..., k, None, None], eb)
    return ea[..., :, None, :] * eb[..., None, :, :]


def depth_band(taps, depth, block):
    kt = taps.shape[-1]
    half = (kt - 1) // 2
    i = lax.broadcasted_iota(jnp.int32, (3 * block, block), 0)
    j = lax.broadcasted_iota(jnp.int32, (3 * block, block), 1)
    d = i - block - j + half
    strip = jnp.zeros(taps.shape[:-1] + (3 * block, block), jnp.float32)
    for k in range(kt):
        strip = jnp.where(d == k, taps[..., k, None, None], strip)
    nb = depth // block
    lead = taps.shape[:-1]
    cols = []
    for b in range(nb):
        col = jnp.pad(strip, [(0, 0)] * len(lead) + [(b * block, (nb - 1 - b) * block), (0, 0)])
        cols.append(col[..., block : block + depth, :])
    return jnp.concatenate(cols, axis=-1)


def on_device(estimate, observed, tile_offset, tile_view, psf_taps, view_weight):
    kt = psf_taps.shape[3]
    rim = (kt - 1) // 2
    block_x, block_y, depth = estimate.shape
    tile_count = observed.shape[1]
    tile_rows = observed.shape[2]
    rank_terms = psf_taps.shape[1]
    group_size = lax.axis_size("tile")
    region_rows = block_y * group_size
    win_rows = -(-(tile_rows + 2 * rim) // 8) * 8
    win_x = block_x + 2 * rim

    tile_info = jnp.stack([tile_offset.astype(jnp.float32), view_weight[tile_view]], axis=1)
    all_info = lax.all_gather(tile_info, "tile", tiled=True)
    all_offset = all_info[:, 0].astype(jnp.int32)
    all_weight = all_info[:, 1]

    rimmed = with_halo(estimate, (("region", 0),), rim)
    gathered = lax.all_gather(rimmed, "tile", axis=1, tiled=True)

    filters = psf_taps[tile_view]
    weight = view_weight[tile_view]
    ax = filters[:, :, 0]
    ay = filters[:, :, 1]
    az = filters[:, :, 2]

    starts = jnp.clip(tile_offset - rim, 0, region_rows - win_rows)
    shifts = tile_offset - rim - starts
    windows = jnp.stack(
        [lax.dynamic_slice_in_dim(gathered, starts[j], win_rows, 1) for j in range(tile_count)]
    ).reshape(tile_count, win_x * win_rows, depth)

    kxy = kron_band(ax, ay, block_x, tile_rows, win_rows, win_x * win_rows, 0, shifts[:, None]).reshape(
        tile_count, rank_terms * block_x * tile_rows, win_x * win_rows
    )
    tz = depth_band(az, depth, 128)

    cells = block_x * tile_rows
    part = jnp.einsum("tmk,tkz->tmz", kxy, windows, precision=MATMUL_PRECISION)
    part = part.reshape(tile_count, rank_terms, cells, depth)
    blurred = dot_rounded_data("tqmz,tqzn->tmn", part, tz, True)

    quotient = observed.transpose(1, 0, 2, 3).reshape(tile_count, cells, depth) / blurred

    ry = ay[..., ::-1]
    rx = ax[..., ::-1]
    ci = lax.broadcasted_iota(jnp.int32, (tile_rows, cells), 1)
    fy_d = ci % tile_rows - lax.broadcasted_iota(jnp.int32, (tile_rows, cells), 0) + rim
    fx_d = lax.broadcasted_iota(jnp.int32, (block_x, cells), 1) // tile_rows - lax.broadcasted_iota(
        jnp.int32, (block_x, cells), 0
    ) + rim
    fy_e = jnp.zeros((tile_count, rank_terms, tile_rows, cells), jnp.float32)
    fx_e = jnp.zeros((tile_count, rank_terms, block_x, cells), jnp.float32)
    for k in range(kt):
        fy_e = jnp.where(fy_d == k, ry[..., k, None, None], fy_e)
        fx_e = jnp.where(fx_d == k, rx[..., k, None, None], fx_e)
    fxy = (fy_e[:, :, :, None, :] * fx_e[:, :, None, :, :]).reshape(tile_count, rank_terms * cells, cells)
    part = dot_rounded_data("tmk,tkz->tmz", quotient, fxy, False)
    part = part.reshape(tile_count, rank_terms, cells, depth)
    correction = jnp.einsum("tqmz,tqnz->tmn", part, tz, precision=MATMUL_PRECISION)
    weighted = (weight[:, None, None] * correction).reshape(tile_count, tile_rows, block_x, depth)
    rows_all = lax.broadcasted_iota(jnp.int32, (tile_count, region_rows, tile_rows), 1)
    rows_tile = lax.broadcasted_iota(jnp.int32, (tile_count, region_rows, tile_rows), 2)
    place = (rows_all - rows_tile == tile_offset[:, None, None]).astype(jnp.float32)
    numerator = jnp.einsum("jYy,jyxz->Yxz", place, weighted, precision=MATMUL_PRECISION)
    own_numerator = lax.psum_scatter(numerator, "tile", scatter_dimension=0, tiled=True).transpose(1, 0, 2)

    me = lax.axis_index("tile")
    rows = me * block_y + jnp.arange(block_y, dtype=jnp.int32)
    inside = (rows[None, :] >= all_offset[:, None]) & (rows[None, :] < all_offset[:, None] + tile_rows)
    own_coverage = jnp.sum(jnp.where(inside, all_weight[:, None], 0.0), axis=0)
    return estimate * (own_numerator + PRIOR_WEIGHT) / (own_coverage[None, :, None] + PRIOR_WEIGHT)


def solution(mesh):
    return jax.shard_map(
        on_device,
        mesh=mesh,
        in_specs=(
            P("region", "tile", None),
            P("region", "tile", None, None),
            P("tile"),
            P("tile"),
            P(),
            P(),
        ),
        out_specs=P("region", "tile", None),
        check_vma=False,
    )
```

```python
import jax
import jax.numpy as jnp
from jax import lax
from jax.sharding import PartitionSpec as P

PRIOR_WEIGHT = 0.25
MATMUL_PRECISION = lax.Precision.HIGH


def with_halo(cells, sides, width):
    for axis, dim in sides:
        count = lax.axis_size(axis)
        ends = count - 1
        head = lax.slice_in_dim(cells, 0, width, axis=dim)
        tail = lax.slice_in_dim(cells, cells.shape[dim] - width, cells.shape[dim], axis=dim)
        cells = jnp.concatenate(
            [
                lax.ppermute(tail, axis, [(i, (i + 1) % count) for i in range(ends)]),
                cells,
                lax.ppermute(head, axis, [((i + 1) % count, i) for i in range(ends)]),
            ],
            axis=dim,
        )
    return cells


def split_bf16(values):
    high = lax.reduce_precision(values, exponent_bits=8, mantissa_bits=7)
    return high.astype(jnp.bfloat16), (values - high).astype(jnp.bfloat16)


def dot_rounded_data(spec, data, taps, data_first):
    data_high = data.astype(jnp.bfloat16)
    taps_high, taps_low = split_bf16(taps)
    if data_first:
        terms = [(data_high, taps_high), (data_high, taps_low)]
    else:
        terms = [(taps_high, data_high), (taps_low, data_high)]
    return sum(jnp.einsum(spec, a, b, preferred_element_type=jnp.float32) for a, b in terms)


def kron_band(taps_a, taps_b, rows_a, rows_b, span_b, cols, shift_a, shift_b):
    kt = taps_a.shape[-1]
    lead = taps_a.shape[:-1]
    ia = lax.broadcasted_iota(jnp.int32, (rows_a, cols), 0)
    ca = lax.broadcasted_iota(jnp.int32, (rows_a, cols), 1) // span_b
    ib = lax.broadcasted_iota(jnp.int32, (rows_b, cols), 0)
    cb = lax.broadcasted_iota(jnp.int32, (rows_b, cols), 1) % span_b
    da = ca - ia - jnp.asarray(shift_a, jnp.int32)[..., None, None]
    db = cb - ib - jnp.asarray(shift_b, jnp.int32)[..., None, None]
    ea = jnp.zeros(lead + (rows_a, cols), jnp.float32)
    eb = jnp.zeros(lead + (rows_b, cols), jnp.float32)
    for k in range(kt):
        ea = jnp.where(da == k, taps_a[..., k, None, None], ea)
        eb = jnp.where(db == k, taps_b[..., k, None, None], eb)
    return ea[..., :, None, :] * eb[..., None, :, :]


def depth_band(taps, depth, block):
    kt = taps.shape[-1]
    half = (kt - 1) // 2
    i = lax.broadcasted_iota(jnp.int32, (3 * block, block), 0)
    j = lax.broadcasted_iota(jnp.int32, (3 * block, block), 1)
    d = i - block - j + half
    strip = jnp.zeros(taps.shape[:-1] + (3 * block, block), jnp.float32)
    for k in range(kt):
        strip = jnp.where(d == k, taps[..., k, None, None], strip)
    nb = depth // block
    lead = taps.shape[:-1]
    cols = []
    for b in range(nb):
        col = jnp.pad(strip, [(0, 0)] * len(lead) + [(b * block, (nb - 1 - b) * block), (0, 0)])
        cols.append(col[..., block : block + depth, :])
    return jnp.concatenate(cols, axis=-1)


def on_device(estimate, observed, tile_offset, tile_view, psf_taps, view_weight):
    kt = psf_taps.shape[3]
    rim = (kt - 1) // 2
    block_x, block_y, depth = estimate.shape
    tile_count = observed.shape[1]
    tile_rows = observed.shape[2]
    rank_terms = psf_taps.shape[1]
    group_size = lax.axis_size("tile")
    region_rows = block_y * group_size
    win_rows = -(-(tile_rows + 2 * rim) // 8) * 8
    win_x = block_x + 2 * rim

    tile_info = jnp.stack([tile_offset.astype(jnp.float32), view_weight[tile_view]], axis=1)
    all_info = lax.all_gather(tile_info, "tile", tiled=True)
    all_offset = all_info[:, 0].astype(jnp.int32)
    all_weight = all_info[:, 1]

    rimmed = with_halo(estimate, (("region", 0),), rim)
    gathered = lax.all_gather(rimmed, "tile", axis=1, tiled=True)

    filters = psf_taps[tile_view]
    weight = view_weight[tile_view]
    ax = filters[:, :, 0]
    ay = filters[:, :, 1]
    az = filters[:, :, 2]

    starts = jnp.clip(tile_offset - rim, 0, region_rows - win_rows)
    shifts = tile_offset - rim - starts
    windows = jnp.stack(
        [lax.dynamic_slice_in_dim(gathered, starts[j], win_rows, 1) for j in range(tile_count)]
    ).reshape(tile_count, win_x * win_rows, depth)

    kxy = kron_band(ax, ay, block_x, tile_rows, win_rows, win_x * win_rows, 0, shifts[:, None]).reshape(
        tile_count, rank_terms * block_x * tile_rows, win_x * win_rows
    )
    tz = depth_band(az, depth, 128)

    cells = block_x * tile_rows
    part = jnp.einsum("tmk,tkz->tmz", kxy, windows, precision=MATMUL_PRECISION)
    part = part.reshape(tile_count, rank_terms, cells, depth)
    blurred = dot_rounded_data("tqmz,tqzn->tmn", part, tz, True)

    quotient = observed.transpose(1, 0, 2, 3).reshape(tile_count, cells, depth) / blurred

    ry = ay[..., ::-1]
    rx = ax[..., ::-1]
    ci = lax.broadcasted_iota(jnp.int32, (tile_rows, cells), 1)
    fy_d = ci % tile_rows - lax.broadcasted_iota(jnp.int32, (tile_rows, cells), 0) + rim
    fx_d = lax.broadcasted_iota(jnp.int32, (block_x, cells), 1) // tile_rows - lax.broadcasted_iota(
        jnp.int32, (block_x, cells), 0
    ) + rim
    fy_e = jnp.zeros((tile_count, rank_terms, tile_rows, cells), jnp.float32)
    fx_e = jnp.zeros((tile_count, rank_terms, block_x, cells), jnp.float32)
    for k in range(kt):
        fy_e = jnp.where(fy_d == k, ry[..., k, None, None], fy_e)
        fx_e = jnp.where(fx_d == k, rx[..., k, None, None], fx_e)
    fxy = (fy_e[:, :, :, None, :] * fx_e[:, :, None, :, :]).reshape(tile_count, rank_terms * cells, cells)
    part = dot_rounded_data("tmk,tkz->tmz", quotient, fxy, False)
    part = part.reshape(tile_count, rank_terms, cells, depth)
    correction = jnp.einsum("tqmz,tqnz->tmn", part, tz, precision=MATMUL_PRECISION)
    weighted = (weight[:, None, None] * correction).reshape(tile_count, tile_rows, block_x, depth)
    rows_all = lax.broadcasted_iota(jnp.int32, (tile_count, region_rows, tile_rows), 1)
    rows_tile = lax.broadcasted_iota(jnp.int32, (tile_count, region_rows, tile_rows), 2)
    place = (rows_all - rows_tile == tile_offset[:, None, None]).astype(jnp.float32)
    numerator = jnp.einsum("jYy,jyxz->Yxz", place, weighted, precision=MATMUL_PRECISION)
    own_numerator = lax.psum_scatter(numerator, "tile", scatter_dimension=0, tiled=True).transpose(1, 0, 2)

    me = lax.axis_index("tile")
    rows = me * block_y + jnp.arange(block_y, dtype=jnp.int32)
    inside = (rows[None, :] >= all_offset[:, None]) & (rows[None, :] < all_offset[:, None] + tile_rows)
    own_coverage = jnp.sum(jnp.where(inside, all_weight[:, None], 0.0), axis=0)
    scale = lax.optimization_barrier(estimate / (own_coverage[None, :, None] + PRIOR_WEIGHT))
    return scale * (own_numerator + PRIOR_WEIGHT)


def solution(mesh):
    return jax.shard_map(
        on_device,
        mesh=mesh,
        in_specs=(
            P("region", "tile", None),
            P("region", "tile", None, None),
            P("tile"),
            P("tile"),
            P(),
            P(),
        ),
        out_specs=P("region", "tile", None),
        check_vma=False,
    )
```

```python
import jax
import jax.numpy as jnp
from jax import lax
from jax.sharding import PartitionSpec as P

PRIOR_WEIGHT = 0.25
MATMUL_PRECISION = lax.Precision.HIGH


def with_halo(cells, sides, width):
    for axis, dim in sides:
        count = lax.axis_size(axis)
        ends = count - 1
        head = lax.slice_in_dim(cells, 0, width, axis=dim)
        tail = lax.slice_in_dim(cells, cells.shape[dim] - width, cells.shape[dim], axis=dim)
        cells = jnp.concatenate(
            [
                lax.ppermute(tail, axis, [(i, (i + 1) % count) for i in range(ends)]),
                cells,
                lax.ppermute(head, axis, [((i + 1) % count, i) for i in range(ends)]),
            ],
            axis=dim,
        )
    return cells


def split_bf16(values):
    high = lax.reduce_precision(values, exponent_bits=8, mantissa_bits=7)
    return high.astype(jnp.bfloat16), (values - high).astype(jnp.bfloat16)


def dot_rounded_data(spec, data, taps, data_first):
    data_high = data.astype(jnp.bfloat16)
    taps_high, taps_low = split_bf16(taps)
    if data_first:
        terms = [(data_high, taps_high), (data_high, taps_low)]
    else:
        terms = [(taps_high, data_high), (taps_low, data_high)]
    return sum(jnp.einsum(spec, a, b, preferred_element_type=jnp.float32) for a, b in terms)


def kron_band(taps_a, taps_b, rows_a, rows_b, span_b, cols, shift_a, shift_b):
    kt = taps_a.shape[-1]
    lead = taps_a.shape[:-1]
    ia = lax.broadcasted_iota(jnp.int32, (rows_a, cols), 0)
    ca = lax.broadcasted_iota(jnp.int32, (rows_a, cols), 1) // span_b
    ib = lax.broadcasted_iota(jnp.int32, (rows_b, cols), 0)
    cb = lax.broadcasted_iota(jnp.int32, (rows_b, cols), 1) % span_b
    da = ca - ia - jnp.asarray(shift_a, jnp.int32)[..., None, None]
    db = cb - ib - jnp.asarray(shift_b, jnp.int32)[..., None, None]
    ea = jnp.zeros(lead + (rows_a, cols), jnp.float32)
    eb = jnp.zeros(lead + (rows_b, cols), jnp.float32)
    for k in range(kt):
        ea = jnp.where(da == k, taps_a[..., k, None, None], ea)
        eb = jnp.where(db == k, taps_b[..., k, None, None], eb)
    return ea[..., :, None, :] * eb[..., None, :, :]


def depth_band(taps, depth, block):
    kt = taps.shape[-1]
    half = (kt - 1) // 2
    i = lax.broadcasted_iota(jnp.int32, (3 * block, block), 0)
    j = lax.broadcasted_iota(jnp.int32, (3 * block, block), 1)
    d = i - block - j + half
    strip = jnp.zeros(taps.shape[:-1] + (3 * block, block), jnp.float32)
    for k in range(kt):
        strip = jnp.where(d == k, taps[..., k, None, None], strip)
    nb = depth // block
    lead = taps.shape[:-1]
    cols = []
    for b in range(nb):
        col = jnp.pad(strip, [(0, 0)] * len(lead) + [(b * block, (nb - 1 - b) * block), (0, 0)])
        cols.append(col[..., block : block + depth, :])
    return jnp.concatenate(cols, axis=-1)


def on_device(estimate, observed, tile_offset, tile_view, psf_taps, view_weight):
    kt = psf_taps.shape[3]
    rim = (kt - 1) // 2
    block_x, block_y, depth = estimate.shape
    tile_count = observed.shape[1]
    tile_rows = observed.shape[2]
    rank_terms = psf_taps.shape[1]
    group_size = lax.axis_size("tile")
    region_rows = block_y * group_size
    win_rows = -(-(tile_rows + 2 * rim) // 8) * 8
    win_x = block_x + 2 * rim

    tile_info = jnp.stack([tile_offset.astype(jnp.float32), view_weight[tile_view]], axis=1)
    all_info = lax.all_gather(tile_info, "tile", tiled=True)
    all_offset = all_info[:, 0].astype(jnp.int32)
    all_weight = all_info[:, 1]

    rimmed = with_halo(estimate, (("region", 0),), rim)
    gathered = lax.all_gather(rimmed, "tile", axis=1, tiled=True)

    filters = psf_taps[tile_view]
    weight = view_weight[tile_view]
    ax = filters[:, :, 0]
    ay = filters[:, :, 1]
    az = filters[:, :, 2]

    starts = jnp.clip(tile_offset - rim, 0, region_rows - win_rows)
    shifts = tile_offset - rim - starts
    windows = jnp.stack(
        [lax.dynamic_slice_in_dim(gathered, starts[j], win_rows, 1) for j in range(tile_count)]
    ).reshape(tile_count, win_x * win_rows, depth)

    kxy = kron_band(ax, ay, block_x, tile_rows, win_rows, win_x * win_rows, 0, shifts[:, None]).reshape(
        tile_count, rank_terms * block_x * tile_rows, win_x * win_rows
    )
    tz = depth_band(az, depth, 128)

    cells = block_x * tile_rows
    half_x = block_x // 2
    span_x = half_x + 2 * rim
    kxy6 = kxy.reshape(tile_count, rank_terms, block_x, tile_rows, win_x, win_rows)
    blurred = []
    for g in range(2):
        k_g = kxy6[:, :, g * half_x : (g + 1) * half_x, :, g * half_x : g * half_x + span_x].reshape(
            tile_count, rank_terms * half_x * tile_rows, span_x * win_rows
        )
        w_g = windows[:, g * half_x * win_rows : (g * half_x + span_x) * win_rows]
        part = jnp.einsum("tmk,tkz->tmz", k_g, w_g, precision=MATMUL_PRECISION)
        part = part.reshape(tile_count, rank_terms, half_x * tile_rows, depth)
        blurred.append(dot_rounded_data("tqmz,tqzn->tmn", part, tz, True))
    blurred = jnp.concatenate(blurred, axis=1)

    quotient = observed.transpose(1, 0, 2, 3).reshape(tile_count, cells, depth) / blurred

    ry = ay[..., ::-1]
    rx = ax[..., ::-1]
    ci = lax.broadcasted_iota(jnp.int32, (tile_rows, cells), 1)
    fy_d = ci % tile_rows - lax.broadcasted_iota(jnp.int32, (tile_rows, cells), 0) + rim
    fx_d = lax.broadcasted_iota(jnp.int32, (block_x, cells), 1) // tile_rows - lax.broadcasted_iota(
        jnp.int32, (block_x, cells), 0
    ) + rim
    fy_e = jnp.zeros((tile_count, rank_terms, tile_rows, cells), jnp.float32)
    fx_e = jnp.zeros((tile_count, rank_terms, block_x, cells), jnp.float32)
    for k in range(kt):
        fy_e = jnp.where(fy_d == k, ry[..., k, None, None], fy_e)
        fx_e = jnp.where(fx_d == k, rx[..., k, None, None], fx_e)
    fxy = (fy_e[:, :, :, None, :] * fx_e[:, :, None, :, :]).reshape(tile_count, rank_terms * cells, cells)
    part = dot_rounded_data("tmk,tkz->tmz", quotient, fxy, False)
    part = part.reshape(tile_count, rank_terms, cells, depth)
    correction = jnp.einsum("tqmz,tqnz->tmn", part, tz, precision=MATMUL_PRECISION)
    weighted = (weight[:, None, None] * correction).reshape(tile_count, tile_rows, block_x, depth)
    rows_all = lax.broadcasted_iota(jnp.int32, (tile_count, region_rows, tile_rows), 1)
    rows_tile = lax.broadcasted_iota(jnp.int32, (tile_count, region_rows, tile_rows), 2)
    place = (rows_all - rows_tile == tile_offset[:, None, None]).astype(jnp.float32)
    numerator = jnp.einsum("jYy,jyxz->Yxz", place, weighted, precision=MATMUL_PRECISION)
    own_numerator = lax.psum_scatter(numerator, "tile", scatter_dimension=0, tiled=True).transpose(1, 0, 2)

    me = lax.axis_index("tile")
    rows = me * block_y + jnp.arange(block_y, dtype=jnp.int32)
    inside = (rows[None, :] >= all_offset[:, None]) & (rows[None, :] < all_offset[:, None] + tile_rows)
    own_coverage = jnp.sum(jnp.where(inside, all_weight[:, None], 0.0), axis=0)
    return estimate * (own_numerator + PRIOR_WEIGHT) / (own_coverage[None, :, None] + PRIOR_WEIGHT)


def solution(mesh):
    return jax.shard_map(
        on_device,
        mesh=mesh,
        in_specs=(
            P("region", "tile", None),
            P("region", "tile", None, None),
            P("tile"),
            P("tile"),
            P(),
            P(),
        ),
        out_specs=P("region", "tile", None),
        check_vma=False,
    )
```

```python
import jax
import jax.numpy as jnp
from jax import lax
from jax.sharding import PartitionSpec as P

PRIOR_WEIGHT = 0.25
MATMUL_PRECISION = lax.Precision.HIGH


def with_halo(cells, sides, width):
    for axis, dim in sides:
        count = lax.axis_size(axis)
        ends = count - 1
        head = lax.slice_in_dim(cells, 0, width, axis=dim)
        tail = lax.slice_in_dim(cells, cells.shape[dim] - width, cells.shape[dim], axis=dim)
        cells = jnp.concatenate(
            [
                lax.ppermute(tail, axis, [(i, (i + 1) % count) for i in range(ends)]),
                cells,
                lax.ppermute(head, axis, [((i + 1) % count, i) for i in range(ends)]),
            ],
            axis=dim,
        )
    return cells


def split_bf16(values):
    high = lax.reduce_precision(values, exponent_bits=8, mantissa_bits=7)
    return high.astype(jnp.bfloat16), (values - high).astype(jnp.bfloat16)


def dot_rounded_data(spec, data, taps, data_first):
    data_high = lax.reduce_precision(data, exponent_bits=8, mantissa_bits=7).astype(jnp.bfloat16)
    taps_high, taps_low = split_bf16(taps)
    if data_first:
        terms = [(data_high, taps_high), (data_high, taps_low)]
    else:
        terms = [(taps_high, data_high), (taps_low, data_high)]
    return sum(jnp.einsum(spec, a, b, preferred_element_type=jnp.float32) for a, b in terms)


def kron_band(taps_a, taps_b, rows_a, rows_b, span_b, cols, shift_a, shift_b):
    kt = taps_a.shape[-1]
    lead = taps_a.shape[:-1]
    ia = lax.broadcasted_iota(jnp.int32, (rows_a, cols), 0)
    ca = lax.broadcasted_iota(jnp.int32, (rows_a, cols), 1) // span_b
    ib = lax.broadcasted_iota(jnp.int32, (rows_b, cols), 0)
    cb = lax.broadcasted_iota(jnp.int32, (rows_b, cols), 1) % span_b
    da = ca - ia - jnp.asarray(shift_a, jnp.int32)[..., None, None]
    db = cb - ib - jnp.asarray(shift_b, jnp.int32)[..., None, None]
    ea = jnp.zeros(lead + (rows_a, cols), jnp.float32)
    eb = jnp.zeros(lead + (rows_b, cols), jnp.float32)
    for k in range(kt):
        ea = jnp.where(da == k, taps_a[..., k, None, None], ea)
        eb = jnp.where(db == k, taps_b[..., k, None, None], eb)
    return ea[..., :, None, :] * eb[..., None, :, :]


def depth_band(taps, depth, block):
    kt = taps.shape[-1]
    half = (kt - 1) // 2
    i = lax.broadcasted_iota(jnp.int32, (3 * block, block), 0)
    j = lax.broadcasted_iota(jnp.int32, (3 * block, block), 1)
    d = i - block - j + half
    strip = jnp.zeros(taps.shape[:-1] + (3 * block, block), jnp.float32)
    for k in range(kt):
        strip = jnp.where(d == k, taps[..., k, None, None], strip)
    nb = depth // block
    lead = taps.shape[:-1]
    cols = []
    for b in range(nb):
        col = jnp.pad(strip, [(0, 0)] * len(lead) + [(b * block, (nb - 1 - b) * block), (0, 0)])
        cols.append(col[..., block : block + depth, :])
    return jnp.concatenate(cols, axis=-1)


def on_device(estimate, observed, tile_offset, tile_view, psf_taps, view_weight):
    kt = psf_taps.shape[3]
    rim = (kt - 1) // 2
    block_x, block_y, depth = estimate.shape
    tile_count = observed.shape[1]
    tile_rows = observed.shape[2]
    rank_terms = psf_taps.shape[1]
    group_size = lax.axis_size("tile")
    region_rows = block_y * group_size
    win_rows = -(-(tile_rows + 2 * rim) // 8) * 8
    win_x = block_x + 2 * rim

    tile_info = jnp.stack([tile_offset.astype(jnp.float32), view_weight[tile_view]], axis=1)
    all_info = lax.all_gather(tile_info, "tile", tiled=True)
    all_offset = all_info[:, 0].astype(jnp.int32)
    all_weight = all_info[:, 1]

    rimmed = with_halo(estimate, (("region", 0),), rim)
    gathered = lax.all_gather(rimmed, "tile", axis=1, tiled=True)

    filters = psf_taps[tile_view]
    weight = view_weight[tile_view]
    ax = filters[:, :, 0]
    ay = filters[:, :, 1]
    az = filters[:, :, 2]

    starts = jnp.clip(tile_offset - rim, 0, region_rows - win_rows)
    shifts = tile_offset - rim - starts
    windows = jnp.stack(
        [lax.dynamic_slice_in_dim(gathered, starts[j], win_rows, 1) for j in range(tile_count)]
    ).reshape(tile_count, win_x * win_rows, depth)

    kxy = kron_band(ax, ay, block_x, tile_rows, win_rows, win_x * win_rows, 0, shifts[:, None]).reshape(
        tile_count, rank_terms * block_x * tile_rows, win_x * win_rows
    )
    tz = depth_band(az, depth, 128)

    cells = block_x * tile_rows
    part = dot_rounded_data("tmk,tkz->tmz", windows, kxy, False)
    part = part.reshape(tile_count, rank_terms, cells, depth)
    blurred = dot_rounded_data("tqmz,tqzn->tmn", part, tz, True)

    quotient = observed.transpose(1, 0, 2, 3).reshape(tile_count, cells, depth) / blurred

    ry = ay[..., ::-1]
    rx = ax[..., ::-1]
    ci = lax.broadcasted_iota(jnp.int32, (tile_rows, cells), 1)
    fy_d = ci % tile_rows - lax.broadcasted_iota(jnp.int32, (tile_rows, cells), 0) + rim
    fx_d = lax.broadcasted_iota(jnp.int32, (block_x, cells), 1) // tile_rows - lax.broadcasted_iota(
        jnp.int32, (block_x, cells), 0
    ) + rim
    fy_e = jnp.zeros((tile_count, rank_terms, tile_rows, cells), jnp.float32)
    fx_e = jnp.zeros((tile_count, rank_terms, block_x, cells), jnp.float32)
    for k in range(kt):
        fy_e = jnp.where(fy_d == k, ry[..., k, None, None], fy_e)
        fx_e = jnp.where(fx_d == k, rx[..., k, None, None], fx_e)
    fxy = (fy_e[:, :, :, None, :] * fx_e[:, :, None, :, :]).reshape(tile_count, rank_terms * cells, cells)
    part = dot_rounded_data("tmk,tkz->tmz", quotient, fxy, False)
    part = part.reshape(tile_count, rank_terms, cells, depth)
    correction = jnp.einsum("tqmz,tqnz->tmn", part, tz, precision=MATMUL_PRECISION)
    weighted = (weight[:, None, None] * correction).reshape(tile_count, tile_rows, block_x, depth)
    rows_all = lax.broadcasted_iota(jnp.int32, (tile_count, region_rows, tile_rows), 1)
    rows_tile = lax.broadcasted_iota(jnp.int32, (tile_count, region_rows, tile_rows), 2)
    place = (rows_all - rows_tile == tile_offset[:, None, None]).astype(jnp.float32)
    numerator = jnp.einsum("jYy,jyxz->Yxz", place, weighted, precision=MATMUL_PRECISION)
    own_numerator = lax.psum_scatter(numerator, "tile", scatter_dimension=0, tiled=True).transpose(1, 0, 2)

    me = lax.axis_index("tile")
    rows = me * block_y + jnp.arange(block_y, dtype=jnp.int32)
    inside = (rows[None, :] >= all_offset[:, None]) & (rows[None, :] < all_offset[:, None] + tile_rows)
    own_coverage = jnp.sum(jnp.where(inside, all_weight[:, None], 0.0), axis=0)
    return estimate * (own_numerator + PRIOR_WEIGHT) / (own_coverage[None, :, None] + PRIOR_WEIGHT)


def solution(mesh):
    return jax.shard_map(
        on_device,
        mesh=mesh,
        in_specs=(
            P("region", "tile", None),
            P("region", "tile", None, None),
            P("tile"),
            P("tile"),
            P(),
            P(),
        ),
        out_specs=P("region", "tile", None),
        check_vma=False,
    )
```

```python
import jax
import jax.numpy as jnp
from jax import lax
from jax.sharding import PartitionSpec as P

PRIOR_WEIGHT = 0.25
MATMUL_PRECISION = lax.Precision.HIGH


def with_halo(cells, sides, width):
    for axis, dim in sides:
        count = lax.axis_size(axis)
        ends = count - 1
        head = lax.slice_in_dim(cells, 0, width, axis=dim)
        tail = lax.slice_in_dim(cells, cells.shape[dim] - width, cells.shape[dim], axis=dim)
        cells = jnp.concatenate(
            [
                lax.ppermute(tail, axis, [(i, (i + 1) % count) for i in range(ends)]),
                cells,
                lax.ppermute(head, axis, [((i + 1) % count, i) for i in range(ends)]),
            ],
            axis=dim,
        )
    return cells


def split_bf16(values):
    high = lax.reduce_precision(values, exponent_bits=8, mantissa_bits=7)
    return high.astype(jnp.bfloat16), (values - high).astype(jnp.bfloat16)


def dot_rounded_data(spec, data, taps, data_first):
    data_high = data.astype(jnp.bfloat16)
    taps_high, taps_low = split_bf16(taps)
    if data_first:
        terms = [(data_high, taps_high), (data_high, taps_low)]
    else:
        terms = [(taps_high, data_high), (taps_low, data_high)]
    return sum(jnp.einsum(spec, a, b, preferred_element_type=jnp.float32) for a, b in terms)


def kron_band(taps_a, taps_b, rows_a, rows_b, span_b, cols, shift_a, shift_b):
    kt = taps_a.shape[-1]
    lead = taps_a.shape[:-1]
    ia = lax.broadcasted_iota(jnp.int32, (rows_a, cols), 0)
    ca = lax.broadcasted_iota(jnp.int32, (rows_a, cols), 1) // span_b
    ib = lax.broadcasted_iota(jnp.int32, (rows_b, cols), 0)
    cb = lax.broadcasted_iota(jnp.int32, (rows_b, cols), 1) % span_b
    da = ca - ia - jnp.asarray(shift_a, jnp.int32)[..., None, None]
    db = cb - ib - jnp.asarray(shift_b, jnp.int32)[..., None, None]
    ea = jnp.zeros(lead + (rows_a, cols), jnp.float32)
    eb = jnp.zeros(lead + (rows_b, cols), jnp.float32)
    for k in range(kt):
        ea = jnp.where(da == k, taps_a[..., k, None, None], ea)
        eb = jnp.where(db == k, taps_b[..., k, None, None], eb)
    return ea[..., :, None, :] * eb[..., None, :, :]


def depth_band(taps, depth, block):
    kt = taps.shape[-1]
    half = (kt - 1) // 2
    i = lax.broadcasted_iota(jnp.int32, (3 * block, block), 0)
    j = lax.broadcasted_iota(jnp.int32, (3 * block, block), 1)
    d = i - block - j + half
    strip = jnp.zeros(taps.shape[:-1] + (3 * block, block), jnp.float32)
    for k in range(kt):
        strip = jnp.where(d == k, taps[..., k, None, None], strip)
    nb = depth // block
    lead = taps.shape[:-1]
    cols = []
    for b in range(nb):
        col = jnp.pad(strip, [(0, 0)] * len(lead) + [(b * block, (nb - 1 - b) * block), (0, 0)])
        cols.append(col[..., block : block + depth, :])
    return jnp.concatenate(cols, axis=-1)


def on_device(estimate, observed, tile_offset, tile_view, psf_taps, view_weight):
    kt = psf_taps.shape[3]
    rim = (kt - 1) // 2
    block_x, block_y, depth = estimate.shape
    tile_count = observed.shape[1]
    tile_rows = observed.shape[2]
    rank_terms = psf_taps.shape[1]
    group_size = lax.axis_size("tile")
    region_rows = block_y * group_size
    win_rows = -(-(tile_rows + 2 * rim) // 8) * 8
    win_x = block_x + 2 * rim

    tile_info = jnp.stack([tile_offset.astype(jnp.float32), view_weight[tile_view]], axis=1)
    all_info = lax.all_gather(tile_info, "tile", tiled=True)
    all_offset = all_info[:, 0].astype(jnp.int32)
    all_weight = all_info[:, 1]

    rimmed = with_halo(estimate, (("region", 0),), rim)
    gathered = lax.all_gather(rimmed, "tile", axis=1, tiled=True)

    filters = psf_taps[tile_view]
    weight = view_weight[tile_view]
    ax = filters[:, :, 0]
    ay = filters[:, :, 1]
    az = filters[:, :, 2]

    starts = jnp.clip(tile_offset - rim, 0, region_rows - win_rows)
    shifts = tile_offset - rim - starts
    windows = jnp.stack(
        [lax.dynamic_slice_in_dim(gathered, starts[j], win_rows, 1) for j in range(tile_count)]
    ).reshape(tile_count, win_x * win_rows, depth)

    kxy = kron_band(ax, ay, block_x, tile_rows, win_rows, win_x * win_rows, 0, shifts[:, None]).reshape(
        tile_count, rank_terms * block_x * tile_rows, win_x * win_rows
    )
    tz = depth_band(az, depth, 128)

    cells = block_x * tile_rows
    part = jnp.einsum("tmk,tkz->tmz", kxy, windows, precision=MATMUL_PRECISION)
    part = part.reshape(tile_count, rank_terms, cells, depth)
    blurred = dot_rounded_data("tqmz,tqzn->tmn", part, tz, True)

    quotient = observed.transpose(1, 0, 2, 3).reshape(tile_count, cells, depth) / blurred

    ry = ay[..., ::-1]
    rx = ax[..., ::-1]
    ci = lax.broadcasted_iota(jnp.int32, (tile_rows, cells), 1)
    fy_d = ci % tile_rows - lax.broadcasted_iota(jnp.int32, (tile_rows, cells), 0) + rim
    fx_d = lax.broadcasted_iota(jnp.int32, (block_x, cells), 1) // tile_rows - lax.broadcasted_iota(
        jnp.int32, (block_x, cells), 0
    ) + rim
    fy_e = jnp.zeros((tile_count, rank_terms, tile_rows, cells), jnp.float32)
    fx_e = jnp.zeros((tile_count, rank_terms, block_x, cells), jnp.float32)
    for k in range(kt):
        fy_e = jnp.where(fy_d == k, ry[..., k, None, None], fy_e)
        fx_e = jnp.where(fx_d == k, rx[..., k, None, None], fx_e)
    fxy = (fy_e[:, :, :, None, :] * fx_e[:, :, None, :, :]).reshape(tile_count, rank_terms * cells, cells)
    part = dot_rounded_data("tmk,tkz->tmz", quotient, fxy, False)
    part = part.reshape(tile_count, rank_terms, cells, depth)
    correction = jnp.einsum("tqmz,tqnz->tmn", part, tz, precision=MATMUL_PRECISION)
    weighted = (weight[:, None, None] * correction).reshape(tile_count, tile_rows, block_x, depth)
    rows_all = lax.broadcasted_iota(jnp.int32, (tile_count, region_rows, tile_rows), 1)
    rows_tile = lax.broadcasted_iota(jnp.int32, (tile_count, region_rows, tile_rows), 2)
    place = (rows_all - rows_tile == tile_offset[:, None, None]).astype(jnp.float32)
    data_hi, data_lo = split_bf16(weighted)
    place = place.astype(jnp.bfloat16)
    numerator = sum(
        jnp.einsum("jYy,jyxz->Yxz", place, d, preferred_element_type=jnp.float32) for d in (data_hi, data_lo)
    )
    own_numerator = lax.psum_scatter(numerator, "tile", scatter_dimension=0, tiled=True).transpose(1, 0, 2)

    me = lax.axis_index("tile")
    rows = me * block_y + jnp.arange(block_y, dtype=jnp.int32)
    inside = (rows[None, :] >= all_offset[:, None]) & (rows[None, :] < all_offset[:, None] + tile_rows)
    own_coverage = jnp.sum(jnp.where(inside, all_weight[:, None], 0.0), axis=0)
    return estimate * (own_numerator + PRIOR_WEIGHT) / (own_coverage[None, :, None] + PRIOR_WEIGHT)


def solution(mesh):
    return jax.shard_map(
        on_device,
        mesh=mesh,
        in_specs=(
            P("region", "tile", None),
            P("region", "tile", None, None),
            P("tile"),
            P("tile"),
            P(),
            P(),
        ),
        out_specs=P("region", "tile", None),
        check_vma=False,
    )
```
